32 devices in a mesh: leaf: 8 (over z, y), panel: 4 (over x, core).
Axes of the slice: x: 2, y: 2, z: 4, core: 2. Of those that a mesh axis runs over, the one named last changes fastest.
Arguments:
- interface_block: float32 [8, 2048, 2048], P('leaf', 'panel'), may hold values from -0.125 to 0.125
- coupling: bfloat16 [8, 2048, 128], P('leaf', 'panel'), may hold values from -0.375 to 0.375
- eigenvalues: float32 [8, 128], P('leaf'), may hold values from 0.5 to 8
- mode_counts: int32 [8], P('leaf'), may hold values from 64 to 128, as said below
- interface_coords: bfloat16 [8, 2048, 1024], P('leaf', 'panel'), may hold values from -6 to 6
- modal_coords: bfloat16 [8, 128, 4096], P('leaf'), may hold values from -6 to 6
Outputs:
- mode_shapes: float32 [8, 2048, 1024], P('leaf', 'panel')
The draws below stay inside these ranges and needn't reach their ends.
Inputs may be any that keep to these rules, and one draw needn't show every extreme that they name: `mode_counts`: modes kept by each substructure; some substructure keeps all 128.
All inputs are finite; a program needn't handle non-finite values.
Results may differ from the reference program's by a relative error of at most 0.0023.
Values may be sent and summed in bfloat16 or wider, within the bound.
No kernel may reach another device: no remote copies, remote signals or barrier semaphores. Data moves between devices by JAX's collectives and lax.ppermute only.
A program may use at most 128 MiB of HBM per device.

```python
import math
import jax
import jax.numpy as jnp
from jax import lax

NI = 2048
M = 128
RL = 1024
LEAVES = 8
GROUP = 4


def draw_mode_counts(key, part):
    first, second = jax.random.split(key)
    counts = jax.random.randint(first, (LEAVES,), M // 2, M + 1)
    where = jax.random.randint(second, (), 0, LEAVES)
    return counts.at[where].set(M).astype(jnp.int32)


def block_levels(rng, extent, cuts, low, top_value):
    factor_of, own = 1.0, jax.random.fold_in(rng, 6)
    for axis_at, shards_of in cuts:
        draws = jnp.exp(jax.random.uniform(jax.random.fold_in(own, axis_at), (shards_of,), jnp.float32, low / len(cuts), top_value / len(cuts)))
        factor_of = factor_of * jnp.repeat(draws, extent[axis_at] // shards_of).reshape([-1 if axis == axis_at else 1 for axis in range(len(extent))])
    return factor_of


def normal_values(own_key, dims, spread, most, cuts=(), kind=jnp.bfloat16):
    factor_of = block_levels(own_key, dims, cuts, -0.22, 0.18) if cuts else 1.0
    array = jax.random.normal(own_key, dims, jnp.float32) * spread * factor_of
    return jnp.minimum(jnp.maximum(array, -most), most).astype(kind)


def setup_inputs(seed: int = 0) -> dict:
    key_list = jax.random.split(jax.random.key(seed), 7)
    return {
        "interface_block": normal_values(key_list[0], (LEAVES, NI, NI), NI ** -0.5, 0.125, ((0, 8), (1, 4)), jnp.float32),
        "coupling": normal_values(key_list[1], (LEAVES, NI, M), (2 * M) ** -0.5, 0.375, ((0, 8), (1, 4))),
        "eigenvalues": jnp.clip(jnp.exp(math.log(8.0) - 2.7725887 * jax.random.uniform(key_list[2], (LEAVES, M), jnp.float32) ** block_levels(key_list[2], (LEAVES, M), ((0, 8),), -0.2, 0.2)), 0.5, 8.0),
        "mode_counts": draw_mode_counts(jax.random.fold_in(key_list[6], 71), 0),
        "interface_coords": normal_values(key_list[4], (LEAVES, NI, RL), 1.0, 6.0, ((0, 8), (1, 4))),
        "modal_coords": normal_values(key_list[5], (LEAVES, M, GROUP * RL), 1.0, 6.0, ((0, 8),)),
    }


def group_shapes(packed):
    block4, coup4, lam4, count4, coords4, modal4 = packed
    index = jnp.arange(M, dtype=jnp.int32)
    mask = (index[None, :] < count4[:, None]).astype(jnp.float32)
    scaled = (coup4.astype(jnp.float32) * (mask / lam4)[:, None, :]).astype(jnp.bfloat16)
    product = jnp.einsum("lim,ljm->lij", scaled.astype(jnp.float32), coup4.astype(jnp.float32))
    merged = jnp.sum(block4 - product, axis=0)
    modal_term = jnp.einsum("lik,lkc->ic", scaled.astype(jnp.float32), modal4.astype(jnp.float32))
    modal_term = jnp.transpose(modal_term.reshape(NI, GROUP, RL), (1, 0, 2))
    shapes = jnp.einsum("ij,ljr->lir", merged, coords4.astype(jnp.float32), precision=lax.Precision.HIGHEST)
    return shapes + modal_term


def reference(interface_block, coupling, eigenvalues, mode_counts, interface_coords, modal_coords):
    groups = LEAVES // GROUP
    packed = (interface_block.reshape(groups, GROUP, NI, NI),
              coupling.reshape(groups, GROUP, NI, M),
              eigenvalues.reshape(groups, GROUP, M),
              mode_counts.reshape(groups, GROUP),
              interface_coords.reshape(groups, GROUP, NI, RL),
              modal_coords.reshape(groups, GROUP, M, GROUP * RL))
    result = lax.map(group_shapes, packed)
    return result.reshape(LEAVES, NI, RL)
```

```python
import jax
import jax.numpy as jnp
from jax import lax
from jax.sharding import Mesh, PartitionSpec as P


def on_device(interface_block, coupling, eigenvalues, mode_counts, interface_coords, modal_coords):
    block = interface_block[0]
    coup = coupling[0]
    coords = interface_coords[0]
    modal = modal_coords[0]
    width = coup.shape[1]
    group = lax.axis_size("leafin")
    index = jnp.arange(width, dtype=jnp.int32)
    mask = (index < mode_counts[0]).astype(jnp.float32)
    scaled = (coup.astype(jnp.float32) * (mask / eigenvalues[0])[None, :]).astype(jnp.bfloat16)
    dense = lax.psum(block, "leafin")
    scaled_all = lax.all_gather(scaled, "leafin", axis=1, tiled=True)
    coup_rows = lax.all_gather(coup, "panel", axis=0, tiled=True)
    coup_all = lax.all_gather(coup_rows, "leafin", axis=1, tiled=True)
    low = lax.dot_general(scaled_all, coup_all, (((1,), (1,)), ((), ())), preferred_element_type=jnp.float32)
    merged = dense - low
    rl = modal.shape[1] // group
    parts = jnp.transpose(modal.reshape(modal.shape[0], group, rl), (1, 0, 2))
    recv = lax.all_to_all(parts, "leafin", 0, 0, tiled=True)
    modal_term = jnp.dot(scaled_all, recv.reshape(group * modal.shape[0], rl), preferred_element_type=jnp.float32)
    coords_all = lax.all_gather(coords, "panel", axis=0, tiled=True)
    shapes = modal_term + jnp.dot(merged, coords_all.astype(jnp.float32), precision=lax.Precision.HIGHEST)
    return shapes[None]


def solution(mesh):
    def run(*args):
        group = args[5].shape[2] // args[4].shape[2]
        leaves, panels = mesh.shape["leaf"], mesh.shape["panel"]
        grid = mesh.devices.reshape(leaves // group, group, panels)
        sub = Mesh(grid, ("grp", "leafin", "panel"))
        leaf = ("grp", "leafin")
        placed = (
            P(leaf, "panel", None),
            P(leaf, "panel", None),
            P(leaf, None),
            P(leaf),
            P(leaf, "panel", None),
            P(leaf, None, None),
        )
        body = jax.shard_map(on_device, mesh=sub, in_specs=placed, out_specs=P(leaf, "panel", None), check_vma=False)
        return body(*args)

    return run
```

```python
import jax
import jax.numpy as jnp
from jax import lax
from jax.sharding import Mesh, PartitionSpec as P

F32, BF16 = jnp.float32, jnp.bfloat16


def swap(value, axis, mask):
    return lax.ppermute(value, axis, [(i, i ^ mask) for i in range(lax.axis_size(axis))])


def bit_of(axis, bit):
    return (lax.axis_index(axis) >> bit) & 1


def halves(stack, bit, axis=0):
    keep = lax.dynamic_index_in_dim(stack, bit, axis, keepdims=False)
    send = lax.dynamic_index_in_dim(stack, 1 - bit, axis, keepdims=False)
    return keep, send


def place(mine, other, bit, axis=0):
    return jnp.where(bit == 0, jnp.stack([mine, other], axis), jnp.stack([other, mine], axis))


def gather_bits(value, axis):
    bits = (lax.axis_size(axis) - 1).bit_length()
    out = value[None]
    for level, bit in enumerate(range(bits - 1, -1, -1)):
        other = swap(out, axis, 1 << bit)
        out = place(out, other, bit_of(axis, bit), axis=level)
    return out.reshape((-1,) + value.shape[1:])


def reduce_scatter_2d(x, first):
    second = 1 - first
    keep, send = halves(x, bit_of("leafin", first), axis=1 - first)
    acc = keep + swap(send, "leafin", 1 << first)
    keep, send = halves(acc, bit_of("leafin", second), axis=0)
    return keep + swap(send, "leafin", 1 << second)


def all_gather_2d(piece, first):
    last = 1 - first
    got = place(piece, swap(piece, "leafin", 1 << last), bit_of("leafin", last))
    return place(got, swap(got, "leafin", 1 << first), bit_of("leafin", first), axis=1 - first)


def on_device(interface_block, coupling, eigenvalues, mode_counts, interface_coords, modal_coords):
    block = interface_block[0]
    coup = coupling[0]
    coords = interface_coords[0]
    modal = modal_coords[0]
    rows, width = coup.shape
    cols = block.shape[1]
    group = lax.axis_size("leafin")
    me = lax.axis_index("leafin")
    index = jnp.arange(width, dtype=jnp.int32)
    mask = (index < mode_counts[0]).astype(F32)
    scaled = (coup.astype(F32) * (mask / eigenvalues[0])[None, :]).astype(BF16)

    coup_all = gather_bits(coup, "panel")
    schur = block - lax.dot_general(scaled, coup_all, (((1,), (1,)), ((), ())), preferred_element_type=F32)

    half = rows // 2
    piece = half // group
    merged = []
    for h in range(2):
        part = schur[h * half:(h + 1) * half].reshape(2, 2, piece, cols)
        summed = reduce_scatter_2d(part, h)
        merged.append(all_gather_2d(summed, h).reshape(half, cols))
    merged = jnp.concatenate(merged, axis=0)

    rl = modal.shape[1] // group
    modal3 = modal.reshape(modal.shape[0], group, rl)
    lhs, rhs = [scaled], [lax.dynamic_index_in_dim(modal3, me, 1, keepdims=False)]
    for d in range(1, group):
        lhs.append(swap(scaled, "leafin", d))
        rhs.append(swap(lax.dynamic_index_in_dim(modal3, me ^ d, 1, keepdims=False), "leafin", d))
    modal_term = jnp.dot(jnp.concatenate(lhs, axis=1), jnp.concatenate(rhs, axis=0), preferred_element_type=F32)

    coords_all = gather_bits(coords, "panel")
    hi = merged.astype(BF16)
    rest = merged - hi.astype(F32)
    mid = rest.astype(BF16)
    lo = (rest - mid.astype(F32)).astype(BF16)
    product = jnp.dot(lo, coords_all, preferred_element_type=F32) + jnp.dot(mid, coords_all, preferred_element_type=F32)
    product = product + jnp.dot(hi, coords_all, preferred_element_type=F32)
    return (modal_term + product)[None]


def solution(mesh):
    def run(*args):
        group = args[5].shape[2] // args[4].shape[2]
        leaves, panels = mesh.shape["leaf"], mesh.shape["panel"]
        grid = mesh.devices.reshape(leaves // group, group, panels)
        sub = Mesh(grid, ("grp", "leafin", "panel"))
        leaf = ("grp", "leafin")
        placed = (
            P(leaf, "panel", None),
            P(leaf, "panel", None),
            P(leaf, None),
            P(leaf),
            P(leaf, "panel", None),
            P(leaf, None, None),
        )
        body = jax.shard_map(on_device, mesh=sub, in_specs=placed, out_specs=P(leaf, "panel", None), check_vma=False)
        return body(*args)

    return run
```

```python
import jax
import jax.numpy as jnp
from jax import lax
from jax.sharding import Mesh, PartitionSpec as P

F32, BF16 = jnp.float32, jnp.bfloat16


def swap(value, axis, mask):
    return lax.ppermute(value, axis, [(i, i ^ mask) for i in range(lax.axis_size(axis))])


def bit_of(axis, bit):
    return (lax.axis_index(axis) >> bit) & 1


def halves(stack, bit, axis=0):
    keep = lax.dynamic_index_in_dim(stack, bit, axis, keepdims=False)
    send = lax.dynamic_index_in_dim(stack, 1 - bit, axis, keepdims=False)
    return keep, send


def place(mine, other, bit, axis=0):
    return jnp.where(bit == 0, jnp.stack([mine, other], axis), jnp.stack([other, mine], axis))


def gather_bits(value, axis):
    bits = (lax.axis_size(axis) - 1).bit_length()
    out = value[None]
    for level, bit in enumerate(range(bits - 1, -1, -1)):
        other = swap(out, axis, 1 << bit)
        out = place(out, other, bit_of(axis, bit), axis=level)
    return out.reshape((-1,) + value.shape[1:])


def reduce_scatter_2d(x, first):
    second = 1 - first
    keep, send = halves(x, bit_of("leafin", first), axis=1 - first)
    acc = keep + swap(send, "leafin", 1 << first)
    keep, send = halves(acc, bit_of("leafin", second), axis=0)
    return keep + swap(send, "leafin", 1 << second)


def all_gather_2d(piece, first):
    last = 1 - first
    got = place(piece, swap(piece, "leafin", 1 << last), bit_of("leafin", last))
    return place(got, swap(got, "leafin", 1 << first), bit_of("leafin", first), axis=1 - first)


def on_device(interface_block, coupling, eigenvalues, mode_counts, interface_coords, modal_coords):
    block = interface_block[0]
    coup = coupling[0]
    coords = interface_coords[0]
    modal = modal_coords[0]
    rows, width = coup.shape
    cols = block.shape[1]
    group = lax.axis_size("leafin")
    me = lax.axis_index("leafin")
    index = jnp.arange(width, dtype=jnp.int32)
    mask = (index < mode_counts[0]).astype(F32)
    scaled = (coup.astype(F32) * (mask / eigenvalues[0])[None, :]).astype(BF16)

    coup_all = gather_bits(coup, "panel")
    schur = block - lax.dot_general(scaled, coup_all, (((1,), (1,)), ((), ())), preferred_element_type=F32)

    half = rows // 2
    piece = half // group
    merged = []
    for h in range(2):
        part = schur[h * half:(h + 1) * half].reshape(2, 2, piece, cols)
        summed = reduce_scatter_2d(part, h)
        merged.append(all_gather_2d(summed, h).reshape(half, cols))
    merged = jnp.concatenate(merged, axis=0)

    rl = modal.shape[1] // group
    modal3 = modal.reshape(modal.shape[0], group, rl)
    lhs, rhs = [scaled], [lax.dynamic_index_in_dim(modal3, me, 1, keepdims=False)]
    for d in range(1, group):
        lhs.append(swap(scaled, "leafin", d))
        rhs.append(swap(lax.dynamic_index_in_dim(modal3, me ^ d, 1, keepdims=False), "leafin", d))
    modal_term = jnp.dot(jnp.concatenate(lhs, axis=1), jnp.concatenate(rhs, axis=0), preferred_element_type=F32)

    coords_all = gather_bits(coords, "panel")
    top = lax.reduce_precision(merged, exponent_bits=8, mantissa_bits=7)
    rest = merged - top
    middle = lax.reduce_precision(rest, exponent_bits=8, mantissa_bits=7)
    hi, mid, lo = top.astype(BF16), middle.astype(BF16), (rest - middle).astype(BF16)
    product = jnp.dot(lo, coords_all, preferred_element_type=F32) + jnp.dot(mid, coords_all, preferred_element_type=F32)
    product = product + jnp.dot(hi, coords_all, preferred_element_type=F32)
    return (modal_term + product)[None]


def solution(mesh):
    def run(*args):
        group = args[5].shape[2] // args[4].shape[2]
        leaves, panels = mesh.shape["leaf"], mesh.shape["panel"]
        grid = mesh.devices.reshape(leaves // group, group, panels)
        sub = Mesh(grid, ("grp", "leafin", "panel"))
        leaf = ("grp", "leafin")
        placed = (
            P(leaf, "panel", None),
            P(leaf, "panel", None),
            P(leaf, None),
            P(leaf),
            P(leaf, "panel", None),
            P(leaf, None, None),
        )
        body = jax.shard_map(on_device, mesh=sub, in_specs=placed, out_specs=P(leaf, "panel", None), check_vma=False)
        return body(*args)

    return run
```

```python
import jax
import jax.numpy as jnp
from jax import lax
from jax.sharding import Mesh, PartitionSpec as P

F32, BF16 = jnp.float32, jnp.bfloat16


def swap(value, axis, mask):
    return lax.ppermute(value, axis, [(i, i ^ mask) for i in range(lax.axis_size(axis))])


def gather_absolute(value, axis):
    size = lax.axis_size(axis)
    held = {0: value}
    for bit in range((size - 1).bit_length() - 1, -1, -1):
        held.update({r | 1 << bit: swap(v, axis, 1 << bit) for r, v in list(held.items())})
    rel = jnp.stack([held[r] for r in range(size)])
    me = lax.axis_index(axis)
    return jnp.concatenate([lax.dynamic_index_in_dim(rel, q ^ me, 0, keepdims=False) for q in range(size)], 0)


def reorder(x, zb, yb):
    def pick(a, b):
        starts = (0, a, b) + (0,) * (x.ndim - 3)
        sizes = (x.shape[0], 1, 1) + x.shape[3:]
        return lax.dynamic_slice(x, starts, sizes).reshape((x.shape[0],) + x.shape[3:])
    return jnp.stack([jnp.stack([pick(a ^ zb, b ^ yb) for b in (0, 1)], 1) for a in (0, 1)], 1)


def split_dot(lhs, rhs):
    top = lax.reduce_precision(lhs, exponent_bits=8, mantissa_bits=7)
    rest = lhs - top
    middle = lax.reduce_precision(rest, exponent_bits=8, mantissa_bits=7)
    parts = (rest - middle).astype(BF16), middle.astype(BF16), top.astype(BF16)
    total = jnp.dot(parts[0], rhs, preferred_element_type=F32) + jnp.dot(parts[1], rhs, preferred_element_type=F32)
    return total + jnp.dot(parts[2], rhs, preferred_element_type=F32)


def on_device(interface_block, coupling, eigenvalues, mode_counts, interface_coords, modal_coords):
    block = interface_block[0]
    coup = coupling[0]
    coords = interface_coords[0]
    modal = modal_coords[0]
    rows, width = coup.shape
    cols = block.shape[1]
    group = lax.axis_size("leafin")
    me = lax.axis_index("leafin")
    yb, zb = me & 1, (me >> 1) & 1
    index = jnp.arange(width, dtype=jnp.int32)
    mask = (index < mode_counts[0]).astype(F32)
    scaled = (coup.astype(F32) * (mask / eigenvalues[0])[None, :]).astype(BF16)

    rl = modal.shape[1] // group
    modal3 = modal.reshape(modal.shape[0], group, rl)
    lhs, rhs = [scaled], [lax.dynamic_index_in_dim(modal3, me, 1, keepdims=False)]
    for d in range(1, group):
        lhs.append(swap(scaled, "leafin", d))
        rhs.append(swap(lax.dynamic_index_in_dim(modal3, me ^ d, 1, keepdims=False), "leafin", d))

    coup_all = gather_absolute(coup, "panel")
    piece = rows // 8
    blk = reorder(block.reshape(2, 2, 2, piece, cols), zb, yb)
    sc = reorder(scaled.reshape(2, 2, 2, piece, width), zb, yb)
    schur = blk - jnp.einsum("habrk,ck->habrc", sc, coup_all, preferred_element_type=F32)
    schur, lhs, rhs = lax.optimization_barrier((schur, lhs, rhs))

    y, z = 1, 2
    got = {}
    for h, (first, second) in enumerate(((y, z), (z, y))):
        x = schur[h]
        if first == y:
            near = [swap(x[a, 1], "leafin", y) for a in (0, 1)]
            fwd = x[1, 0] + near[1]
            own = x[0, 0] + near[0] + swap(fwd, "leafin", z)
        else:
            near = [swap(x[1, b], "leafin", z) for b in (0, 1)]
            fwd = x[0, 1] + near[1]
            own = x[0, 0] + near[0] + swap(fwd, "leafin", y)
        from_y = swap(own, "leafin", y)
        from_z = swap(own, "leafin", z)
        got[h, 0, 0], got[h, 0, 1], got[h, 1, 0] = own, from_y, from_z
        got[h, 1, 1] = swap(from_z, "leafin", y) if first == y else swap(from_y, "leafin", z)

    coords_all = gather_absolute(coords, "panel")
    early = [(0, 0, 0), (0, 0, 1), (0, 1, 0), (1, 0, 0), (1, 0, 1), (1, 1, 0)]
    late = [(0, 1, 1), (1, 1, 1)]
    out_early = split_dot(jnp.concatenate([got[k] for k in early], 0), coords_all)
    out_late = split_dot(jnp.concatenate([got[k] for k in late], 0), coords_all)
    pieces = {k: out_early[i * piece:(i + 1) * piece] for i, k in enumerate(early)}
    pieces.update({k: out_late[i * piece:(i + 1) * piece] for i, k in enumerate(late)})
    out_rel = jnp.stack([jnp.stack([jnp.stack([pieces[h, a, b] for b in (0, 1)]) for a in (0, 1)]) for h in (0, 1)])
    dense = reorder(out_rel, zb, yb).reshape(rows, -1)

    modal_term = jnp.dot(jnp.concatenate(lhs, axis=1), jnp.concatenate(rhs, axis=0), preferred_element_type=F32)
    return (modal_term + dense)[None]


def solution(mesh):
    def run(*args):
        group = args[5].shape[2] // args[4].shape[2]
        leaves, panels = mesh.shape["leaf"], mesh.shape["panel"]
        grid = mesh.devices.reshape(leaves // group, group, panels)
        sub = Mesh(grid, ("grp", "leafin", "panel"))
        leaf = ("grp", "leafin")
        placed = (
            P(leaf, "panel", None),
            P(leaf, "panel", None),
            P(leaf, None),
            P(leaf),
            P(leaf, "panel", None),
            P(leaf, None, None),
        )
        body = jax.shard_map(on_device, mesh=sub, in_specs=placed, out_specs=P(leaf, "panel", None), check_vma=False)
        return body(*args)

    return run
```

```python
import jax
import jax.numpy as jnp
from jax import lax
from jax.sharding import Mesh, PartitionSpec as P

F32, BF16, F16 = jnp.float32, jnp.bfloat16, jnp.float16
TAG = 128


def swap(value, axis, mask):
    return lax.ppermute(value, axis, [(i, i ^ mask) for i in range(lax.axis_size(axis))])


def bit_of(axis, bit):
    return (lax.axis_index(axis) >> bit) & 1


def halves(stack, bit, axis=0):
    keep = lax.dynamic_index_in_dim(stack, bit, axis, keepdims=False)
    send = lax.dynamic_index_in_dim(stack, 1 - bit, axis, keepdims=False)
    return keep, send


def place(mine, other, bit, axis=0):
    return jnp.where(bit == 0, jnp.stack([mine, other], axis), jnp.stack([other, mine], axis))


def gather_bits(value, axis):
    bits = (lax.axis_size(axis) - 1).bit_length()
    out = value[None]
    for level, bit in enumerate(range(bits - 1, -1, -1)):
        other = swap(out, axis, 1 << bit)
        out = place(out, other, bit_of(axis, bit), axis=level)
    return out.reshape((-1,) + value.shape[1:])


def pack(x):
    top = jnp.max(jnp.abs(x), axis=-1, keepdims=True)
    shift = jnp.clip(jnp.floor(jnp.log2(jnp.maximum(top, 1e-30))), -100.0, 100.0)
    values = (x * jnp.exp2(-shift)).astype(F16)
    return jnp.concatenate([values, jnp.broadcast_to(shift, x.shape[:-1] + (TAG,)).astype(F16)], axis=-1)


def unpack(p):
    cols = p.shape[-1] - TAG
    return p[..., :cols].astype(F32) * jnp.exp2(p[..., cols:cols + 1].astype(F32))


def reduce_scatter_2d(x, first):
    second = 1 - first
    keep, send = halves(x, bit_of("leafin", first), axis=1 - first)
    acc = keep + unpack(swap(pack(send), "leafin", 1 << first))
    keep, send = halves(acc, bit_of("leafin", second), axis=0)
    return keep + unpack(swap(pack(send), "leafin", 1 << second))


def all_gather_2d(piece, first):
    last = 1 - first
    piece = pack(piece)
    got = place(piece, swap(piece, "leafin", 1 << last), bit_of("leafin", last))
    return place(got, swap(got, "leafin", 1 << first), bit_of("leafin", first), axis=1 - first)


def on_device(interface_block, coupling, eigenvalues, mode_counts, interface_coords, modal_coords):
    block = interface_block[0]
    coup = coupling[0]
    coords = interface_coords[0]
    modal = modal_coords[0]
    rows, width = coup.shape
    cols = block.shape[1]
    group = lax.axis_size("leafin")
    me = lax.axis_index("leafin")
    index = jnp.arange(width, dtype=jnp.int32)
    mask = (index < mode_counts[0]).astype(F32)
    scaled = (coup.astype(F32) * (mask / eigenvalues[0])[None, :]).astype(BF16)

    coup_all = gather_bits(coup, "panel")
    schur = block - lax.dot_general(scaled, coup_all, (((1,), (1,)), ((), ())), preferred_element_type=F32)

    rl = modal.shape[1] // group
    modal3 = modal.reshape(modal.shape[0], group, rl)
    lhs, rhs = [scaled], [lax.dynamic_index_in_dim(modal3, me, 1, keepdims=False)]
    for d in range(1, group):
        lhs.append(swap(scaled, "leafin", d))
        rhs.append(swap(lax.dynamic_index_in_dim(modal3, me ^ d, 1, keepdims=False), "leafin", d))
    schur, lhs, rhs = lax.optimization_barrier((schur, lhs, rhs))

    half = rows // 2
    piece = half // group
    merged = []
    for h in range(2):
        part = schur[h * half:(h + 1) * half].reshape(2, 2, piece, cols)
        summed = reduce_scatter_2d(part, h)
        merged.append(unpack(all_gather_2d(summed, h)).reshape(half, cols))
    merged = jnp.concatenate(merged, axis=0)

    modal_term = jnp.dot(jnp.concatenate(lhs, axis=1), jnp.concatenate(rhs, axis=0), preferred_element_type=F32)

    coords_all = gather_bits(coords, "panel")
    top = lax.reduce_precision(merged, exponent_bits=8, mantissa_bits=7)
    rest = merged - top
    middle = lax.reduce_precision(rest, exponent_bits=8, mantissa_bits=7)
    hi, mid, lo = top.astype(BF16), middle.astype(BF16), (rest - middle).astype(BF16)
    product = jnp.dot(lo, coords_all, preferred_element_type=F32) + jnp.dot(mid, coords_all, preferred_element_type=F32)
    product = product + jnp.dot(hi, coords_all, preferred_element_type=F32)
    return (modal_term + product)[None]


def solution(mesh):
    def run(*args):
        group = args[5].shape[2] // args[4].shape[2]
        leaves, panels = mesh.shape["leaf"], mesh.shape["panel"]
        grid = mesh.devices.reshape(leaves // group, group, panels)
        sub = Mesh(grid, ("grp", "leafin", "panel"))
        leaf = ("grp", "leafin")
        placed = (
            P(leaf, "panel", None),
            P(leaf, "panel", None),
            P(leaf, None),
            P(leaf),
            P(leaf, "panel", None),
            P(leaf, None, None),
        )
        body = jax.shard_map(on_device, mesh=sub, in_specs=placed, out_specs=P(leaf, "panel", None), check_vma=False)
        return body(*args)

    return run
```

```python
import jax
import jax.numpy as jnp
from jax import lax
from jax.sharding import Mesh, PartitionSpec as P

F32, BF16, F16 = jnp.float32, jnp.bfloat16, jnp.float16
TAG = 128


def swap(value, axis, mask):
    return lax.ppermute(value, axis, [(i, i ^ mask) for i in range(lax.axis_size(axis))])


def bit_of(axis, bit):
    return (lax.axis_index(axis) >> bit) & 1


def halves(stack, bit, axis=0):
    keep = lax.dynamic_index_in_dim(stack, bit, axis, keepdims=False)
    send = lax.dynamic_index_in_dim(stack, 1 - bit, axis, keepdims=False)
    return keep, send


def place(mine, other, bit, axis=0):
    return jnp.where(bit == 0, jnp.stack([mine, other], axis), jnp.stack([other, mine], axis))


def gather_bits(value, axis):
    bits = (lax.axis_size(axis) - 1).bit_length()
    out = value[None]
    for level, bit in enumerate(range(bits - 1, -1, -1)):
        other = swap(out, axis, 1 << bit)
        out = place(out, other, bit_of(axis, bit), axis=level)
    return out.reshape((-1,) + value.shape[1:])


def pack(x):
    top = jnp.max(jnp.abs(x), axis=-1, keepdims=True)
    shift = jnp.clip(jnp.floor(jnp.log2(jnp.maximum(top, 1e-30))), -100.0, 100.0)
    values = (x * jnp.exp2(-shift)).astype(F16)
    return jnp.concatenate([values, jnp.broadcast_to(shift, x.shape[:-1] + (TAG,)).astype(F16)], axis=-1)


def unpack(p):
    cols = p.shape[-1] - TAG
    return p[..., :cols].astype(F32) * jnp.exp2(p[..., cols:cols + 1].astype(F32))


def reduce_scatter_2d(x, first):
    second = 1 - first
    keep, send = halves(x, bit_of("leafin", first), axis=1 - first)
    acc = keep + unpack(swap(pack(send), "leafin", 1 << first))
    keep, send = halves(acc, bit_of("leafin", second), axis=0)
    return keep + unpack(swap(pack(send), "leafin", 1 << second))


def all_gather_2d(piece, first):
    last = 1 - first
    piece = pack(piece)
    got = place(piece, swap(piece, "leafin", 1 << last), bit_of("leafin", last))
    return place(got, swap(got, "leafin", 1 << first), bit_of("leafin", first), axis=1 - first)


def on_device(interface_block, coupling, eigenvalues, mode_counts, interface_coords, modal_coords):
    block = interface_block[0]
    coup = coupling[0]
    coords = interface_coords[0]
    modal = modal_coords[0]
    rows, width = coup.shape
    cols = block.shape[1]
    group = lax.axis_size("leafin")
    me = lax.axis_index("leafin")
    index = jnp.arange(width, dtype=jnp.int32)
    mask = (index < mode_counts[0]).astype(F32)
    scaled = (coup.astype(F32) * (mask / eigenvalues[0])[None, :]).astype(BF16)

    coup_all = gather_bits(coup, "panel")
    schur = block - lax.dot_general(scaled, coup_all, (((1,), (1,)), ((), ())), preferred_element_type=F32)

    rl = modal.shape[1] // group
    schur, scaled_late, modal_late = lax.optimization_barrier((schur, scaled, modal))
    modal3 = modal_late.reshape(modal.shape[0], group, rl)
    lhs, rhs = [scaled_late], [lax.dynamic_index_in_dim(modal3, me, 1, keepdims=False)]
    for d in range(1, group):
        lhs.append(swap(scaled_late, "leafin", d))
        rhs.append(swap(lax.dynamic_index_in_dim(modal3, me ^ d, 1, keepdims=False), "leafin", d))

    half = rows // 2
    piece = half // group
    merged = []
    for h in range(2):
        part = schur[h * half:(h + 1) * half].reshape(2, 2, piece, cols)
        summed = reduce_scatter_2d(part, h)
        merged.append(unpack(all_gather_2d(summed, h)).reshape(half, cols))
    merged = jnp.concatenate(merged, axis=0)

    modal_term = jnp.dot(jnp.concatenate(lhs, axis=1), jnp.concatenate(rhs, axis=0), preferred_element_type=F32)

    coords_all = gather_bits(coords, "panel")
    top = lax.reduce_precision(merged, exponent_bits=8, mantissa_bits=7)
    hi, lo = top.astype(BF16), (merged - top).astype(BF16)
    product = jnp.dot(lo, coords_all, preferred_element_type=F32) + jnp.dot(hi, coords_all, preferred_element_type=F32)
    return (modal_term + product)[None]


def solution(mesh):
    def run(*args):
        group = args[5].shape[2] // args[4].shape[2]
        leaves, panels = mesh.shape["leaf"], mesh.shape["panel"]
        grid = mesh.devices.reshape(leaves // group, group, panels)
        sub = Mesh(grid, ("grp", "leafin", "panel"))
        leaf = ("grp", "leafin")
        placed = (
            P(leaf, "panel", None),
            P(leaf, "panel", None),
            P(leaf, None),
            P(leaf),
            P(leaf, "panel", None),
            P(leaf, None, None),
        )
        body = jax.shard_map(on_device, mesh=sub, in_specs=placed, out_specs=P(leaf, "panel", None), check_vma=False)
        return body(*args)

    return run
```

```python
import jax
import jax.numpy as jnp
from jax import lax
from jax.sharding import Mesh, PartitionSpec as P

F32, BF16, F16 = jnp.float32, jnp.bfloat16, jnp.float16
TAG = 128


def swap(value, axis, mask):
    return lax.ppermute(value, axis, [(i, i ^ mask) for i in range(lax.axis_size(axis))])


def bit_of(axis, bit):
    return (lax.axis_index(axis) >> bit) & 1


def halves(stack, bit, axis=0):
    keep = lax.dynamic_index_in_dim(stack, bit, axis, keepdims=False)
    send = lax.dynamic_index_in_dim(stack, 1 - bit, axis, keepdims=False)
    return keep, send


def place(mine, other, bit, axis=0):
    return jnp.where(bit == 0, jnp.stack([mine, other], axis), jnp.stack([other, mine], axis))


def gather_direct(value, axis):
    size = lax.axis_size(axis)
    me = lax.axis_index(axis)
    rel = jnp.stack([value] + [swap(value, axis, d) for d in range(1, size)])
    return jnp.concatenate([lax.dynamic_index_in_dim(rel, q ^ me, 0, keepdims=False) for q in range(size)], 0)


def gather_bits(value, axis):
    bits = (lax.axis_size(axis) - 1).bit_length()
    out = value[None]
    for level, bit in enumerate(range(bits - 1, -1, -1)):
        other = swap(out, axis, 1 << bit)
        out = place(out, other, bit_of(axis, bit), axis=level)
    return out.reshape((-1,) + value.shape[1:])


def pack(x):
    top = jnp.max(jnp.abs(x), axis=-1, keepdims=True)
    shift = jnp.clip(jnp.floor(jnp.log2(jnp.maximum(top, 1e-30))), -100.0, 100.0)
    values = (x * jnp.exp2(-shift)).astype(F16)
    return jnp.concatenate([values, jnp.broadcast_to(shift, x.shape[:-1] + (TAG,)).astype(F16)], axis=-1)


def unpack(p):
    cols = p.shape[-1] - TAG
    return p[..., :cols].astype(F32) * jnp.exp2(p[..., cols:cols + 1].astype(F32))


def reduce_scatter_2d(x, first):
    second = 1 - first
    keep, send = halves(x, bit_of("leafin", first), axis=1 - first)
    acc = keep + unpack(swap(pack(send), "leafin", 1 << first))
    keep, send = halves(acc, bit_of("leafin", second), axis=0)
    return keep + unpack(swap(pack(send), "leafin", 1 << second))


def all_gather_2d(piece, first):
    last = 1 - first
    piece = pack(piece)
    got = place(piece, swap(piece, "leafin", 1 << last), bit_of("leafin", last))
    return place(got, swap(got, "leafin", 1 << first), bit_of("leafin", first), axis=1 - first)


def on_device(interface_block, coupling, eigenvalues, mode_counts, interface_coords, modal_coords):
    block = interface_block[0]
    coup = coupling[0]
    coords = interface_coords[0]
    modal = modal_coords[0]
    rows, width = coup.shape
    cols = block.shape[1]
    group = lax.axis_size("leafin")
    me = lax.axis_index("leafin")
    index = jnp.arange(width, dtype=jnp.int32)
    mask = (index < mode_counts[0]).astype(F32)
    scaled = (coup.astype(F32) * (mask / eigenvalues[0])[None, :]).astype(BF16)

    coup_all = gather_direct(coup, "panel")
    rl = modal.shape[1] // group
    coup_all, scaled_late, modal_late = lax.optimization_barrier((coup_all, scaled, modal))
    schur = block - lax.dot_general(scaled, coup_all, (((1,), (1,)), ((), ())), preferred_element_type=F32)
    modal3 = modal_late.reshape(modal.shape[0], group, rl)
    lhs, rhs = [scaled_late], [lax.dynamic_index_in_dim(modal3, me, 1, keepdims=False)]
    for d in range(1, group):
        lhs.append(swap(scaled_late, "leafin", d))
        rhs.append(swap(lax.dynamic_index_in_dim(modal3, me ^ d, 1, keepdims=False), "leafin", d))
    schur, lhs, rhs = lax.optimization_barrier((schur, lhs, rhs))

    half = rows // 2
    piece = half // group
    merged = []
    for h in range(2):
        part = schur[h * half:(h + 1) * half].reshape(2, 2, piece, cols)
        summed = reduce_scatter_2d(part, h)
        merged.append(unpack(all_gather_2d(summed, h)).reshape(half, cols))
    merged = jnp.concatenate(merged, axis=0)

    modal_term = jnp.dot(jnp.concatenate(lhs, axis=1), jnp.concatenate(rhs, axis=0), preferred_element_type=F32)

    coords_all = gather_bits(coords, "panel")
    top = lax.reduce_precision(merged, exponent_bits=8, mantissa_bits=7)
    hi, lo = top.astype(BF16), (merged - top).astype(BF16)
    product = jnp.dot(lo, coords_all, preferred_element_type=F32) + jnp.dot(hi, coords_all, preferred_element_type=F32)
    return (modal_term + product)[None]


def solution(mesh):
    def run(*args):
        group = args[5].shape[2] // args[4].shape[2]
        leaves, panels = mesh.shape["leaf"], mesh.shape["panel"]
        grid = mesh.devices.reshape(leaves // group, group, panels)
        sub = Mesh(grid, ("grp", "leafin", "panel"))
        leaf = ("grp", "leafin")
        placed = (
            P(leaf, "panel", None),
            P(leaf, "panel", None),
            P(leaf, None),
            P(leaf),
            P(leaf, "panel", None),
            P(leaf, None, None),
        )
        body = jax.shard_map(on_device, mesh=sub, in_specs=placed, out_specs=P(leaf, "panel", None), check_vma=False)
        return body(*args)

    return run
```

```python
import jax
import jax.numpy as jnp
from jax import lax
from jax.sharding import Mesh, PartitionSpec as P

F32, BF16, F16 = jnp.float32, jnp.bfloat16, jnp.float16
TAG = 128


def swap(value, axis, mask):
    return lax.ppermute(value, axis, [(i, i ^ mask) for i in range(lax.axis_size(axis))])


def bit_of(axis, bit):
    return (lax.axis_index(axis) >> bit) & 1


def halves(stack, bit, axis=0):
    keep = lax.dynamic_index_in_dim(stack, bit, axis, keepdims=False)
    send = lax.dynamic_index_in_dim(stack, 1 - bit, axis, keepdims=False)
    return keep, send


def place(mine, other, bit, axis=0):
    return jnp.where(bit == 0, jnp.stack([mine, other], axis), jnp.stack([other, mine], axis))


def gather_direct(value, axis):
    size = lax.axis_size(axis)
    me = lax.axis_index(axis)
    rel = jnp.stack([value] + [swap(value, axis, d) for d in range(1, size)])
    return jnp.concatenate([lax.dynamic_index_in_dim(rel, q ^ me, 0, keepdims=False) for q in range(size)], 0)


def gather_bits(value, axis):
    bits = (lax.axis_size(axis) - 1).bit_length()
    out = value[None]
    for level, bit in enumerate(range(bits - 1, -1, -1)):
        other = swap(out, axis, 1 << bit)
        out = place(out, other, bit_of(axis, bit), axis=level)
    return out.reshape((-1,) + value.shape[1:])


def pack(x):
    top = jnp.max(jnp.abs(x), axis=-1, keepdims=True)
    shift = jnp.clip(jnp.floor(jnp.log2(jnp.maximum(top, 1e-30))), -100.0, 100.0)
    values = (x * jnp.exp2(-shift)).astype(F16)
    return jnp.concatenate([values, jnp.broadcast_to(shift, x.shape[:-1] + (TAG,)).astype(F16)], axis=-1)


def unpack(p):
    cols = p.shape[-1] - TAG
    return p[..., :cols].astype(F32) * jnp.exp2(p[..., cols:cols + 1].astype(F32))


def reduce_scatter_2d(x, first):
    second = 1 - first
    keep, send = halves(x, bit_of("leafin", first), axis=1 - first)
    acc = keep + unpack(swap(pack(send), "leafin", 1 << first))
    keep, send = halves(acc, bit_of("leafin", second), axis=0)
    return keep + unpack(swap(pack(send), "leafin", 1 << second))


def all_gather_2d(piece, first):
    last = 1 - first
    piece = pack(piece)
    got = place(piece, swap(piece, "leafin", 1 << last), bit_of("leafin", last))
    return place(got, swap(got, "leafin", 1 << first), bit_of("leafin", first), axis=1 - first)


def on_device(interface_block, coupling, eigenvalues, mode_counts, interface_coords, modal_coords):
    block = interface_block[0]
    coup = coupling[0]
    coords = interface_coords[0]
    modal = modal_coords[0]
    rows, width = coup.shape
    cols = block.shape[1]
    group = lax.axis_size("leafin")
    me = lax.axis_index("leafin")
    index = jnp.arange(width, dtype=jnp.int32)
    mask = (index < mode_counts[0]).astype(F32)
    scaled = (coup.astype(F32) * (mask / eigenvalues[0])[None, :]).astype(BF16)

    coup_all = gather_direct(coup, "panel")
    rl = modal.shape[1] // group
    coup_all, scaled_late, modal_late = lax.optimization_barrier((coup_all, scaled, modal))
    schur = block - lax.dot_general(scaled, coup_all, (((1,), (1,)), ((), ())), preferred_element_type=F32)
    quarter = modal.shape[0] // lax.axis_size("panel")
    mine = lax.dynamic_slice_in_dim(modal_late, lax.axis_index("panel") * quarter, quarter, 0)
    modal3 = mine.reshape(quarter, group, rl)
    lhs, rhs = [scaled_late], [lax.dynamic_index_in_dim(modal3, me, 1, keepdims=False)]
    for d in range(1, group):
        lhs.append(swap(scaled_late, "leafin", d))
        rhs.append(swap(lax.dynamic_index_in_dim(modal3, me ^ d, 1, keepdims=False), "leafin", d))
    schur, lhs, rhs = lax.optimization_barrier((schur, lhs, rhs))

    half = rows // 2
    piece = half // group
    merged = []
    for h in range(2):
        part = schur[h * half:(h + 1) * half].reshape(2, 2, piece, cols)
        summed = reduce_scatter_2d(part, h)
        if h == 0:
            summed, late_rhs = lax.optimization_barrier((summed, jnp.stack(rhs)))
        merged.append(unpack(all_gather_2d(summed, h)).reshape(half, cols))
    merged = jnp.concatenate(merged, axis=0)

    full = gather_direct(late_rhs, "panel").reshape(-1, group, quarter, rl)
    full = jnp.transpose(full, (1, 0, 2, 3)).reshape(group * modal.shape[0], rl)
    modal_term = jnp.dot(jnp.concatenate(lhs, axis=1), full, preferred_element_type=F32)

    coords_all = gather_bits(coords, "panel")
    top = lax.reduce_precision(merged, exponent_bits=8, mantissa_bits=7)
    hi, lo = top.astype(BF16), (merged - top).astype(BF16)
    product = jnp.dot(lo, coords_all, preferred_element_type=F32) + jnp.dot(hi, coords_all, preferred_element_type=F32)
    return (modal_term + product)[None]


def solution(mesh):
    def run(*args):
        group = args[5].shape[2] // args[4].shape[2]
        leaves, panels = mesh.shape["leaf"], mesh.shape["panel"]
        grid = mesh.devices.reshape(leaves // group, group, panels)
        sub = Mesh(grid, ("grp", "leafin", "panel"))
        leaf = ("grp", "leafin")
        placed = (
            P(leaf, "panel", None),
            P(leaf, "panel", None),
            P(leaf, None),
            P(leaf),
            P(leaf, "panel", None),
            P(leaf, None, None),
        )
        body = jax.shard_map(on_device, mesh=sub, in_specs=placed, out_specs=P(leaf, "panel", None), check_vma=False)
        return body(*args)

    return run
```

```python
import jax
import jax.numpy as jnp
from jax import lax
from jax.sharding import Mesh, PartitionSpec as P

F32, BF16, F16 = jnp.float32, jnp.bfloat16, jnp.float16
TAG = 128


def swap(value, axis, mask):
    return lax.ppermute(value, axis, [(i, i ^ mask) for i in range(lax.axis_size(axis))])


def bit_of(axis, bit):
    return (lax.axis_index(axis) >> bit) & 1


def halves(stack, bit, axis=0):
    keep = lax.dynamic_index_in_dim(stack, bit, axis, keepdims=False)
    send = lax.dynamic_index_in_dim(stack, 1 - bit, axis, keepdims=False)
    return keep, send


def place(mine, other, bit, axis=0):
    return jnp.where(bit == 0, jnp.stack([mine, other], axis), jnp.stack([other, mine], axis))


def gather_direct(value, axis):
    size = lax.axis_size(axis)
    me = lax.axis_index(axis)
    rel = jnp.stack([value] + [swap(value, axis, d) for d in range(1, size)])
    return jnp.concatenate([lax.dynamic_index_in_dim(rel, q ^ me, 0, keepdims=False) for q in range(size)], 0)


def gather_bits(value, axis):
    bits = (lax.axis_size(axis) - 1).bit_length()
    out = value[None]
    for level, bit in enumerate(range(bits - 1, -1, -1)):
        other = swap(out, axis, 1 << bit)
        out = place(out, other, bit_of(axis, bit), axis=level)
    return out.reshape((-1,) + value.shape[1:])


def pack(x):
    top = jnp.max(jnp.abs(x), axis=-1, keepdims=True)
    shift = jnp.clip(jnp.floor(jnp.log2(jnp.maximum(top, 1e-30))), -100.0, 100.0)
    values = (x * jnp.exp2(-shift)).astype(F16)
    return jnp.concatenate([values, jnp.broadcast_to(shift, x.shape[:-1] + (TAG,)).astype(F16)], axis=-1)


def unpack(p):
    cols = p.shape[-1] - TAG
    return p[..., :cols].astype(F32) * jnp.exp2(p[..., cols:cols + 1].astype(F32))


def reduce_scatter_2d(x, first):
    second = 1 - first
    keep, send = halves(x, bit_of("leafin", first), axis=1 - first)
    acc = keep + unpack(swap(pack(send), "leafin", 1 << first))
    keep, send = halves(acc, bit_of("leafin", second), axis=0)
    return keep + unpack(swap(pack(send), "leafin", 1 << second))


def all_gather_2d(piece, first):
    last = 1 - first
    piece = pack(piece)
    got = place(piece, swap(piece, "leafin", 1 << last), bit_of("leafin", last))
    return place(got, swap(got, "leafin", 1 << first), bit_of("leafin", first), axis=1 - first)


def on_device(interface_block, coupling, eigenvalues, mode_counts, interface_coords, modal_coords):
    block = interface_block[0]
    coup = coupling[0]
    coords = interface_coords[0]
    modal = modal_coords[0]
    rows, width = coup.shape
    cols = block.shape[1]
    group = lax.axis_size("leafin")
    me = lax.axis_index("leafin")
    index = jnp.arange(width, dtype=jnp.int32)
    mask = (index < mode_counts[0]).astype(F32)
    scaled = (coup.astype(F32) * (mask / eigenvalues[0])[None, :]).astype(BF16)

    coup_all = gather_direct(coup, "panel")
    rl = modal.shape[1] // group
    coup_all, scaled_late, modal_late = lax.optimization_barrier((coup_all, scaled, modal))
    schur = block - lax.dot_general(scaled, coup_all, (((1,), (1,)), ((), ())), preferred_element_type=F32)
    quarter = modal.shape[0] // lax.axis_size("panel")
    mine = lax.dynamic_slice_in_dim(modal_late, lax.axis_index("panel") * quarter, quarter, 0)
    modal3 = mine.reshape(quarter, group, rl)
    own_part = lax.dynamic_index_in_dim(modal3, me, 1, keepdims=False)
    lhs, rhs = [scaled_late], [own_part]
    for d in range(1, group):
        part = lax.dynamic_index_in_dim(modal3, me ^ d, 1, keepdims=False).reshape(-1, width)
        got = swap(jnp.concatenate([scaled_late, part], axis=0), "leafin", d)
        lhs.append(got[:rows])
        rhs.append(got[rows:].reshape(own_part.shape))
    schur, lhs, rhs = lax.optimization_barrier((schur, lhs, rhs))

    coords_all = gather_direct(coords, "panel")
    half = rows // 2
    piece = half // group
    outs = []
    late_rhs = jnp.stack(rhs)
    for h in range(2):
        part = schur[h * half:(h + 1) * half].reshape(2, 2, piece, cols)
        summed = pack(reduce_scatter_2d(part, h))
        last = 1 - h
        got = place(summed, swap(summed, "leafin", 1 << last), bit_of("leafin", last))
        if h == 1:
            got, late_rhs = lax.optimization_barrier((got, late_rhs))
        more = swap(got, "leafin", 1 << h)
        early_out = product(unpack(got).reshape(2 * piece, cols), coords_all).reshape(2, piece, -1)
        late_out = product(unpack(more).reshape(2 * piece, cols), coords_all).reshape(2, piece, -1)
        outs.append(place(early_out, late_out, bit_of("leafin", h), axis=1 - h).reshape(half, -1))
    dense = jnp.concatenate(outs, axis=0)

    full = gather_direct(late_rhs, "panel").reshape(-1, group, quarter, rl)
    full = jnp.transpose(full, (1, 0, 2, 3)).reshape(group * modal.shape[0], rl)
    modal_term = jnp.dot(jnp.concatenate(lhs, axis=1), full, preferred_element_type=F32)
    return (modal_term + dense)[None]


def product(lhs, rhs):
    top = lax.reduce_precision(lhs, exponent_bits=8, mantissa_bits=7)
    hi, lo = top.astype(BF16), (lhs - top).astype(BF16)
    return jnp.dot(lo, rhs, preferred_element_type=F32) + jnp.dot(hi, rhs, preferred_element_type=F32)


def solution(mesh):
    def run(*args):
        group = args[5].shape[2] // args[4].shape[2]
        leaves, panels = mesh.shape["leaf"], mesh.shape["panel"]
        grid = mesh.devices.reshape(leaves // group, group, panels)
        sub = Mesh(grid, ("grp", "leafin", "panel"))
        leaf = ("grp", "leafin")
        placed = (
            P(leaf, "panel", None),
            P(leaf, "panel", None),
            P(leaf, None),
            P(leaf),
            P(leaf, "panel", None),
            P(leaf, None, None),
        )
        body = jax.shard_map(on_device, mesh=sub, in_specs=placed, out_specs=P(leaf, "panel", None), check_vma=False)
        return body(*args)

    return run
```

```python
import jax
import jax.numpy as jnp
from jax import lax
from jax.sharding import Mesh, PartitionSpec as P

F32, BF16, F16 = jnp.float32, jnp.bfloat16, jnp.float16
TAG = 128


def swap(value, axis, mask):
    return lax.ppermute(value, axis, [(i, i ^ mask) for i in range(lax.axis_size(axis))])


def bit_of(axis, bit):
    return (lax.axis_index(axis) >> bit) & 1


def halves(stack, bit, axis=0):
    keep = lax.dynamic_index_in_dim(stack, bit, axis, keepdims=False)
    send = lax.dynamic_index_in_dim(stack, 1 - bit, axis, keepdims=False)
    return keep, send


def place(mine, other, bit, axis=0):
    return jnp.where(bit == 0, jnp.stack([mine, other], axis), jnp.stack([other, mine], axis))


def gather_direct(value, axis):
    size = lax.axis_size(axis)
    me = lax.axis_index(axis)
    rel = jnp.stack([value] + [swap(value, axis, d) for d in range(1, size)])
    return jnp.concatenate([lax.dynamic_index_in_dim(rel, q ^ me, 0, keepdims=False) for q in range(size)], 0)


def gather_bits(value, axis):
    bits = (lax.axis_size(axis) - 1).bit_length()
    out = value[None]
    for level, bit in enumerate(range(bits - 1, -1, -1)):
        other = swap(out, axis, 1 << bit)
        out = place(out, other, bit_of(axis, bit), axis=level)
    return out.reshape((-1,) + value.shape[1:])


def pack(x):
    top = jnp.max(jnp.abs(x), axis=-1, keepdims=True)
    shift = jnp.clip(jnp.floor(jnp.log2(jnp.maximum(top, 1e-30))), -100.0, 100.0)
    values = (x * jnp.exp2(-shift)).astype(F16)
    return jnp.concatenate([values, jnp.broadcast_to(shift, x.shape[:-1] + (TAG,)).astype(F16)], axis=-1)


def unpack(p):
    cols = p.shape[-1] - TAG
    return p[..., :cols].astype(F32) * jnp.exp2(p[..., cols:cols + 1].astype(F32))


def reduce_scatter_2d(x, first):
    second = 1 - first
    keep, send = halves(x, bit_of("leafin", first), axis=1 - first)
    acc = keep + unpack(swap(pack(send), "leafin", 1 << first))
    keep, send = halves(acc, bit_of("leafin", second), axis=0)
    return keep + unpack(swap(pack(send), "leafin", 1 << second))


def all_gather_2d(piece, first):
    last = 1 - first
    piece = pack(piece)
    got = place(piece, swap(piece, "leafin", 1 << last), bit_of("leafin", last))
    return place(got, swap(got, "leafin", 1 << first), bit_of("leafin", first), axis=1 - first)


def on_device(interface_block, coupling, eigenvalues, mode_counts, interface_coords, modal_coords):
    block = interface_block[0]
    coup = coupling[0]
    coords = interface_coords[0]
    modal = modal_coords[0]
    rows, width = coup.shape
    cols = block.shape[1]
    group = lax.axis_size("leafin")
    me = lax.axis_index("leafin")
    index = jnp.arange(width, dtype=jnp.int32)
    mask = (index < mode_counts[0]).astype(F32)
    scaled = (coup.astype(F32) * (mask / eigenvalues[0])[None, :]).astype(BF16)

    coup_all = gather_direct(coup, "panel")
    rl = modal.shape[1] // group
    coup_all, scaled_late, modal_late = lax.optimization_barrier((coup_all, scaled, modal))
    schur = block - lax.dot_general(scaled, coup_all, (((1,), (1,)), ((), ())), preferred_element_type=F32)
    quarter = modal.shape[0] // lax.axis_size("panel")
    mine = lax.dynamic_slice_in_dim(modal_late, lax.axis_index("panel") * quarter, quarter, 0)
    modal3 = mine.reshape(quarter, group, rl)
    own_part = lax.dynamic_index_in_dim(modal3, me, 1, keepdims=False)
    lhs, rhs = [scaled_late], [own_part]
    for d in range(1, group):
        part = lax.dynamic_index_in_dim(modal3, me ^ d, 1, keepdims=False).reshape(-1, width)
        got = swap(jnp.concatenate([scaled_late, part], axis=0), "leafin", d)
        lhs.append(got[:rows])
        rhs.append(got[rows:].reshape(own_part.shape))
    schur, lhs, rhs = lax.optimization_barrier((schur, lhs, rhs))

    coords_all = gather_bits(coords, "panel")
    half = rows // 2
    piece = half // group
    outs = []
    late_rhs = jnp.stack(rhs)
    for h in range(2):
        part = schur[h * half:(h + 1) * half].reshape(2, 2, piece, cols)
        summed = pack(reduce_scatter_2d(part, h))
        last = 1 - h
        got = place(summed, swap(summed, "leafin", 1 << last), bit_of("leafin", last))
        if h == 1:
            got, late_rhs = lax.optimization_barrier((got, late_rhs))
        more = swap(got, "leafin", 1 << h)
        early_out = product(unpack(got).reshape(2 * piece, cols), coords_all).reshape(2, piece, -1)
        late_out = product(unpack(more).reshape(2 * piece, cols), coords_all).reshape(2, piece, -1)
        outs.append(place(early_out, late_out, bit_of("leafin", h), axis=1 - h).reshape(half, -1))
    dense = jnp.concatenate(outs, axis=0)

    full = gather_direct(late_rhs, "panel").reshape(-1, group, quarter, rl)
    full = jnp.transpose(full, (1, 0, 2, 3)).reshape(group * modal.shape[0], rl)
    modal_term = jnp.dot(jnp.concatenate(lhs, axis=1), full, preferred_element_type=F32)
    return (modal_term + dense)[None]


def product(lhs, rhs):
    top = lax.reduce_precision(lhs, exponent_bits=8, mantissa_bits=7)
    hi, lo = top.astype(BF16), (lhs - top).astype(BF16)
    return jnp.dot(lo, rhs, preferred_element_type=F32) + jnp.dot(hi, rhs, preferred_element_type=F32)


def solution(mesh):
    def run(*args):
        group = args[5].shape[2] // args[4].shape[2]
        leaves, panels = mesh.shape["leaf"], mesh.shape["panel"]
        grid = mesh.devices.reshape(leaves // group, group, panels)
        sub = Mesh(grid, ("grp", "leafin", "panel"))
        leaf = ("grp", "leafin")
        placed = (
            P(leaf, "panel", None),
            P(leaf, "panel", None),
            P(leaf, None),
            P(leaf),
            P(leaf, "panel", None),
            P(leaf, None, None),
        )
        body = jax.shard_map(on_device, mesh=sub, in_specs=placed, out_specs=P(leaf, "panel", None), check_vma=False)
        return body(*args)

    return run
```

```python
import jax
import jax.numpy as jnp
from jax import lax
from jax.sharding import Mesh, PartitionSpec as P

F32, BF16, F16 = jnp.float32, jnp.bfloat16, jnp.float16
TAG = 128


def swap(value, axis, mask):
    return lax.ppermute(value, axis, [(i, i ^ mask) for i in range(lax.axis_size(axis))])


def bit_of(axis, bit):
    return (lax.axis_index(axis) >> bit) & 1


def halves(stack, bit, axis=0):
    keep = lax.dynamic_index_in_dim(stack, bit, axis, keepdims=False)
    send = lax.dynamic_index_in_dim(stack, 1 - bit, axis, keepdims=False)
    return keep, send


def place(mine, other, bit, axis=0):
    return jnp.where(bit == 0, jnp.stack([mine, other], axis), jnp.stack([other, mine], axis))


def gather_direct(value, axis):
    size = lax.axis_size(axis)
    me = lax.axis_index(axis)
    rel = jnp.stack([value] + [swap(value, axis, d) for d in range(1, size)])
    return jnp.concatenate([lax.dynamic_index_in_dim(rel, q ^ me, 0, keepdims=False) for q in range(size)], 0)


def gather_bits(value, axis):
    bits = (lax.axis_size(axis) - 1).bit_length()
    out = value[None]
    for level, bit in enumerate(range(bits - 1, -1, -1)):
        other = swap(out, axis, 1 << bit)
        out = place(out, other, bit_of(axis, bit), axis=level)
    return out.reshape((-1,) + value.shape[1:])


def pack(x):
    top = jnp.max(jnp.abs(x), axis=-1, keepdims=True)
    shift = jnp.clip(jnp.floor(jnp.log2(jnp.maximum(top, 1e-30))), -100.0, 100.0)
    values = (x * jnp.exp2(-shift)).astype(F16)
    return jnp.concatenate([values, jnp.broadcast_to(shift, x.shape[:-1] + (TAG,)).astype(F16)], axis=-1)


def unpack(p):
    cols = p.shape[-1] - TAG
    return p[..., :cols].astype(F32) * jnp.exp2(p[..., cols:cols + 1].astype(F32))


def reduce_scatter_2d(x, first):
    second = 1 - first
    keep, send = halves(x, bit_of("leafin", first), axis=1 - first)
    acc = keep + unpack(swap(pack(send), "leafin", 1 << first))
    keep, send = halves(acc, bit_of("leafin", second), axis=0)
    return keep + unpack(swap(pack(send), "leafin", 1 << second))


def all_gather_2d(piece, first):
    last = 1 - first
    piece = pack(piece)
    got = place(piece, swap(piece, "leafin", 1 << last), bit_of("leafin", last))
    return place(got, swap(got, "leafin", 1 << first), bit_of("leafin", first), axis=1 - first)


def on_device(interface_block, coupling, eigenvalues, mode_counts, interface_coords, modal_coords):
    block = interface_block[0]
    coup = coupling[0]
    coords = interface_coords[0]
    modal = modal_coords[0]
    rows, width = coup.shape
    cols = block.shape[1]
    group = lax.axis_size("leafin")
    me = lax.axis_index("leafin")
    index = jnp.arange(width, dtype=jnp.int32)
    mask = (index < mode_counts[0]).astype(F32)
    scaled = (coup.astype(F32) * (mask / eigenvalues[0])[None, :]).astype(BF16)

    coup_all = gather_direct(coup, "panel")
    rl = modal.shape[1] // group
    coup_all, scaled_late, modal_late = lax.optimization_barrier((coup_all, scaled, modal))
    schur = block - lax.dot_general(scaled, coup_all, (((1,), (1,)), ((), ())), preferred_element_type=F32)
    quarter = modal.shape[0] // lax.axis_size("panel")
    mine = lax.dynamic_slice_in_dim(modal_late, lax.axis_index("panel") * quarter, quarter, 0)
    modal3 = mine.reshape(quarter, group, rl)
    lhs, rhs = [scaled_late], [lax.dynamic_index_in_dim(modal3, me, 1, keepdims=False)]
    for d in range(1, group):
        lhs.append(swap(scaled_late, "leafin", d))
        rhs.append(swap(lax.dynamic_index_in_dim(modal3, me ^ d, 1, keepdims=False), "leafin", d))
    schur, lhs, rhs = lax.optimization_barrier((schur, lhs, rhs))

    half = rows // 2
    piece = half // group
    merged = []
    for h in range(2):
        part = schur[h * half:(h + 1) * half].reshape(2, 2, piece, cols)
        summed = reduce_scatter_2d(part, h)
        merged.append(unpack(all_gather_2d(summed, h)).reshape(half, cols))
    merged = jnp.concatenate(merged, axis=0)
    merged, late_rhs = lax.optimization_barrier((merged, jnp.stack(rhs)))

    full = gather_direct(late_rhs, "panel").reshape(-1, group, quarter, rl)
    full = jnp.transpose(full, (1, 0, 2, 3)).reshape(group * modal.shape[0], rl)
    modal_term = jnp.dot(jnp.concatenate(lhs, axis=1), full, preferred_element_type=F32)

    coords_all = gather_bits(coords, "panel")
    top = lax.reduce_precision(merged, exponent_bits=8, mantissa_bits=7)
    hi, lo = top.astype(BF16), (merged - top).astype(BF16)
    product = jnp.dot(lo, coords_all, preferred_element_type=F32) + jnp.dot(hi, coords_all, preferred_element_type=F32)
    return (modal_term + product)[None]


def solution(mesh):
    def run(*args):
        group = args[5].shape[2] // args[4].shape[2]
        leaves, panels = mesh.shape["leaf"], mesh.shape["panel"]
        grid = mesh.devices.reshape(leaves // group, group, panels)
        sub = Mesh(grid, ("grp", "leafin", "panel"))
        leaf = ("grp", "leafin")
        placed = (
            P(leaf, "panel", None),
            P(leaf, "panel", None),
            P(leaf, None),
            P(leaf),
            P(leaf, "panel", None),
            P(leaf, None, None),
        )
        body = jax.shard_map(on_device, mesh=sub, in_specs=placed, out_specs=P(leaf, "panel", None), check_vma=False)
        return body(*args)

    return run
```

```python
import jax
import jax.numpy as jnp
from jax import lax
from jax.sharding import Mesh, PartitionSpec as P

F32, BF16, F16 = jnp.float32, jnp.bfloat16, jnp.float16
TAG = 128


def swap(value, axis, mask):
    return lax.ppermute(value, axis, [(i, i ^ mask) for i in range(lax.axis_size(axis))])


def bit_of(axis, bit):
    return (lax.axis_index(axis) >> bit) & 1


def halves(stack, bit, axis=0):
    keep = lax.dynamic_index_in_dim(stack, bit, axis, keepdims=False)
    send = lax.dynamic_index_in_dim(stack, 1 - bit, axis, keepdims=False)
    return keep, send


def place(mine, other, bit, axis=0):
    return jnp.where(bit == 0, jnp.stack([mine, other], axis), jnp.stack([other, mine], axis))


def gather_direct(value, axis):
    size = lax.axis_size(axis)
    me = lax.axis_index(axis)
    rel = jnp.stack([value] + [swap(value, axis, d) for d in range(1, size)])
    return jnp.concatenate([lax.dynamic_index_in_dim(rel, q ^ me, 0, keepdims=False) for q in range(size)], 0)


def gather_bits(value, axis):
    bits = (lax.axis_size(axis) - 1).bit_length()
    out = value[None]
    for level, bit in enumerate(range(bits - 1, -1, -1)):
        other = swap(out, axis, 1 << bit)
        out = place(out, other, bit_of(axis, bit), axis=level)
    return out.reshape((-1,) + value.shape[1:])


def pack(x):
    top = jnp.max(jnp.abs(x), axis=-1, keepdims=True)
    shift = jnp.clip(jnp.floor(jnp.log2(jnp.maximum(top, 1e-30))), -100.0, 100.0)
    values = (x * jnp.exp2(-shift)).astype(F16)
    return jnp.concatenate([values, jnp.broadcast_to(shift, x.shape[:-1] + (TAG,)).astype(F16)], axis=-1)


def unpack(p):
    cols = p.shape[-1] - TAG
    return p[..., :cols].astype(F32) * jnp.exp2(p[..., cols:cols + 1].astype(F32))


def reduce_scatter_2d(x, first):
    second = 1 - first
    keep, send = halves(x, bit_of("leafin", first), axis=1 - first)
    acc = keep + unpack(swap(pack(send), "leafin", 1 << first))
    keep, send = halves(acc, bit_of("leafin", second), axis=0)
    return keep + unpack(swap(pack(send), "leafin", 1 << second))


def all_gather_2d(piece, first):
    last = 1 - first
    piece = pack(piece)
    got = place(piece, swap(piece, "leafin", 1 << last), bit_of("leafin", last))
    return place(got, swap(got, "leafin", 1 << first), bit_of("leafin", first), axis=1 - first)


def on_device(interface_block, coupling, eigenvalues, mode_counts, interface_coords, modal_coords):
    block = interface_block[0]
    coup = coupling[0]
    coords = interface_coords[0]
    modal = modal_coords[0]
    rows, width = coup.shape
    cols = block.shape[1]
    group = lax.axis_size("leafin")
    me = lax.axis_index("leafin")
    index = jnp.arange(width, dtype=jnp.int32)
    mask = (index < mode_counts[0]).astype(F32)
    scaled = (coup.astype(F32) * (mask / eigenvalues[0])[None, :]).astype(BF16)

    coup_all = gather_direct(coup, "panel")
    rl = modal.shape[1] // group
    coup_all, coords = lax.optimization_barrier((coup_all, coords))
    scaled_late, modal_late = scaled, modal
    schur = block - lax.dot_general(scaled, coup_all, (((1,), (1,)), ((), ())), preferred_element_type=F32)
    modal3 = modal_late.reshape(modal.shape[0], group, rl)
    lhs, rhs = [scaled_late], [lax.dynamic_index_in_dim(modal3, me, 1, keepdims=False)]
    for d in range(1, group):
        lhs.append(swap(scaled_late, "leafin", d))
        rhs.append(swap(lax.dynamic_index_in_dim(modal3, me ^ d, 1, keepdims=False), "leafin", d))
    schur, lhs, rhs = lax.optimization_barrier((schur, lhs, rhs))

    half = rows // 2
    piece = half // group
    merged = []
    for h in range(2):
        part = schur[h * half:(h + 1) * half].reshape(2, 2, piece, cols)
        summed = reduce_scatter_2d(part, h)
        merged.append(unpack(all_gather_2d(summed, h)).reshape(half, cols))
    merged = jnp.concatenate(merged, axis=0)

    modal_term = jnp.dot(jnp.concatenate(lhs, axis=1), jnp.concatenate(rhs, axis=0), preferred_element_type=F32)

    coords_all = gather_bits(coords, "panel")
    top = lax.reduce_precision(merged, exponent_bits=8, mantissa_bits=7)
    hi, lo = top.astype(BF16), (merged - top).astype(BF16)
    product = jnp.dot(lo, coords_all, preferred_element_type=F32) + jnp.dot(hi, coords_all, preferred_element_type=F32)
    return (modal_term + product)[None]


def solution(mesh):
    def run(*args):
        group = args[5].shape[2] // args[4].shape[2]
        leaves, panels = mesh.shape["leaf"], mesh.shape["panel"]
        grid = mesh.devices.reshape(leaves // group, group, panels)
        sub = Mesh(grid, ("grp", "leafin", "panel"))
        leaf = ("grp", "leafin")
        placed = (
            P(leaf, "panel", None),
            P(leaf, "panel", None),
            P(leaf, None),
            P(leaf),
            P(leaf, "panel", None),
            P(leaf, None, None),
        )
        body = jax.shard_map(on_device, mesh=sub, in_specs=placed, out_specs=P(leaf, "panel", None), check_vma=False)
        return body(*args)

    return run
```

```python
import jax
import jax.numpy as jnp
from jax import lax
from jax.sharding import Mesh, PartitionSpec as P

F32, BF16, F16 = jnp.float32, jnp.bfloat16, jnp.float16
TAG = 128


def swap(value, axis, mask):
    return lax.ppermute(value, axis, [(i, i ^ mask) for i in range(lax.axis_size(axis))])


def bit_of(axis, bit):
    return (lax.axis_index(axis) >> bit) & 1


def halves(stack, bit, axis=0):
    keep = lax.dynamic_index_in_dim(stack, bit, axis, keepdims=False)
    send = lax.dynamic_index_in_dim(stack, 1 - bit, axis, keepdims=False)
    return keep, send


def place(mine, other, bit, axis=0):
    return jnp.where(bit == 0, jnp.stack([mine, other], axis), jnp.stack([other, mine], axis))


def gather_direct(value, axis):
    size = lax.axis_size(axis)
    me = lax.axis_index(axis)
    rel = jnp.stack([value] + [swap(value, axis, d) for d in range(1, size)])
    return jnp.concatenate([lax.dynamic_index_in_dim(rel, q ^ me, 0, keepdims=False) for q in range(size)], 0)


def gather_bits(value, axis):
    bits = (lax.axis_size(axis) - 1).bit_length()
    out = value[None]
    for level, bit in enumerate(range(bits - 1, -1, -1)):
        other = swap(out, axis, 1 << bit)
        out = place(out, other, bit_of(axis, bit), axis=level)
    return out.reshape((-1,) + value.shape[1:])


def pack(x):
    top = jnp.max(jnp.abs(x), axis=-1, keepdims=True)
    shift = jnp.clip(jnp.floor(jnp.log2(jnp.maximum(top, 1e-30))), -100.0, 100.0)
    values = (x * jnp.exp2(-shift)).astype(F16)
    return jnp.concatenate([values, jnp.broadcast_to(shift, x.shape[:-1] + (TAG,)).astype(F16)], axis=-1)


def unpack(p):
    cols = p.shape[-1] - TAG
    return p[..., :cols].astype(F32) * jnp.exp2(p[..., cols:cols + 1].astype(F32))


def reduce_scatter_2d(x, first):
    second = 1 - first
    keep, send = halves(x, bit_of("leafin", first), axis=1 - first)
    acc = keep + unpack(swap(pack(send), "leafin", 1 << first))
    keep, send = halves(acc, bit_of("leafin", second), axis=0)
    return keep + unpack(swap(pack(send), "leafin", 1 << second))


def all_gather_2d(piece, first):
    last = 1 - first
    piece = pack(piece)
    got = place(piece, swap(piece, "leafin", 1 << last), bit_of("leafin", last))
    return place(got, swap(got, "leafin", 1 << first), bit_of("leafin", first), axis=1 - first)


def on_device(interface_block, coupling, eigenvalues, mode_counts, interface_coords, modal_coords):
    block = interface_block[0]
    coup = coupling[0]
    coords = interface_coords[0]
    modal = modal_coords[0]
    rows, width = coup.shape
    cols = block.shape[1]
    group = lax.axis_size("leafin")
    me = lax.axis_index("leafin")
    index = jnp.arange(width, dtype=jnp.int32)
    mask = (index < mode_counts[0]).astype(F32)
    scaled = (coup.astype(F32) * (mask / eigenvalues[0])[None, :]).astype(BF16)

    coup_all = gather_direct(coup, "panel")
    rl = modal.shape[1] // group
    coup_all, coords = lax.optimization_barrier((coup_all, coords))
    scaled_late, modal_late = scaled, modal
    schur = block - lax.dot_general(scaled, coup_all, (((1,), (1,)), ((), ())), preferred_element_type=F32)
    modal3 = modal_late.reshape(modal.shape[0], group, rl)
    lhs, rhs = [scaled_late], [lax.dynamic_index_in_dim(modal3, me, 1, keepdims=False)]
    for d in range(1, group):
        lhs.append(swap(scaled_late, "leafin", d))
        rhs.append(swap(lax.dynamic_index_in_dim(modal3, me ^ d, 1, keepdims=False), "leafin", d))
    schur, lhs, rhs = lax.optimization_barrier((schur, lhs, rhs))

    coords_all = gather_bits(coords, "panel")
    half = rows // 2
    piece = half // group
    gots = []
    for h in range(2):
        part = schur[h * half:(h + 1) * half].reshape(2, 2, piece, cols)
        summed = pack(reduce_scatter_2d(part, h))
        last = 1 - h
        gots.append(place(summed, swap(summed, "leafin", 1 << last), bit_of("leafin", last)))
    gots, coords_all = lax.optimization_barrier((gots, coords_all))
    outs = []
    for h in range(2):
        more = swap(gots[h], "leafin", 1 << h)
        early_out = product(unpack(gots[h]).reshape(2 * piece, cols), coords_all).reshape(2, piece, -1)
        late_out = product(unpack(more).reshape(2 * piece, cols), coords_all).reshape(2, piece, -1)
        outs.append(place(early_out, late_out, bit_of("leafin", h), axis=1 - h).reshape(half, -1))
    dense = jnp.concatenate(outs, axis=0)

    modal_term = jnp.dot(jnp.concatenate(lhs, axis=1), jnp.concatenate(rhs, axis=0), preferred_element_type=F32)
    return (modal_term + dense)[None]


def product(lhs, rhs):
    top = lax.reduce_precision(lhs, exponent_bits=8, mantissa_bits=7)
    hi, lo = top.astype(BF16), (lhs - top).astype(BF16)
    return jnp.dot(lo, rhs, preferred_element_type=F32) + jnp.dot(hi, rhs, preferred_element_type=F32)


def solution(mesh):
    def run(*args):
        group = args[5].shape[2] // args[4].shape[2]
        leaves, panels = mesh.shape["leaf"], mesh.shape["panel"]
        grid = mesh.devices.reshape(leaves // group, group, panels)
        sub = Mesh(grid, ("grp", "leafin", "panel"))
        leaf = ("grp", "leafin")
        placed = (
            P(leaf, "panel", None),
            P(leaf, "panel", None),
            P(leaf, None),
            P(leaf),
            P(leaf, "panel", None),
            P(leaf, None, None),
        )
        body = jax.shard_map(on_device, mesh=sub, in_specs=placed, out_specs=P(leaf, "panel", None), check_vma=False)
        return body(*args)

    return run
```

```python
import jax
import jax.numpy as jnp
from jax import lax
from jax.sharding import Mesh, PartitionSpec as P

F32, BF16, F16 = jnp.float32, jnp.bfloat16, jnp.float16
TAG = 128


def swap(value, axis, mask):
    return lax.ppermute(value, axis, [(i, i ^ mask) for i in range(lax.axis_size(axis))])


def bit_of(axis, bit):
    return (lax.axis_index(axis) >> bit) & 1


def halves(stack, bit, axis=0):
    keep = lax.dynamic_index_in_dim(stack, bit, axis, keepdims=False)
    send = lax.dynamic_index_in_dim(stack, 1 - bit, axis, keepdims=False)
    return keep, send


def place(mine, other, bit, axis=0):
    return jnp.where(bit == 0, jnp.stack([mine, other], axis), jnp.stack([other, mine], axis))


def gather_direct(value, axis):
    size = lax.axis_size(axis)
    me = lax.axis_index(axis)
    rel = jnp.stack([value] + [swap(value, axis, d) for d in range(1, size)])
    return jnp.concatenate([lax.dynamic_index_in_dim(rel, q ^ me, 0, keepdims=False) for q in range(size)], 0)


def gather_bits(value, axis):
    bits = (lax.axis_size(axis) - 1).bit_length()
    out = value[None]
    for level, bit in enumerate(range(bits - 1, -1, -1)):
        other = swap(out, axis, 1 << bit)
        out = place(out, other, bit_of(axis, bit), axis=level)
    return out.reshape((-1,) + value.shape[1:])


def pack(x):
    top = jnp.max(jnp.abs(x), axis=-1, keepdims=True)
    shift = jnp.clip(jnp.floor(jnp.log2(jnp.maximum(top, 1e-30))), -100.0, 100.0)
    values = (x * jnp.exp2(-shift)).astype(F16)
    return jnp.concatenate([values, jnp.broadcast_to(shift, x.shape[:-1] + (TAG,)).astype(F16)], axis=-1)


def unpack(p):
    cols = p.shape[-1] - TAG
    return p[..., :cols].astype(F32) * jnp.exp2(p[..., cols:cols + 1].astype(F32))


def reduce_scatter_2d(x, first):
    second = 1 - first
    keep, send = halves(x, bit_of("leafin", first), axis=1 - first)
    acc = keep + unpack(swap(pack(send), "leafin", 1 << first))
    keep, send = halves(acc, bit_of("leafin", second), axis=0)
    return keep + unpack(swap(pack(send), "leafin", 1 << second))


def all_gather_2d(piece, first):
    last = 1 - first
    piece = pack(piece)
    got = place(piece, swap(piece, "leafin", 1 << last), bit_of("leafin", last))
    return place(got, swap(got, "leafin", 1 << first), bit_of("leafin", first), axis=1 - first)


def on_device(interface_block, coupling, eigenvalues, mode_counts, interface_coords, modal_coords):
    block = interface_block[0]
    coup = coupling[0]
    coords = interface_coords[0]
    modal = modal_coords[0]
    rows, width = coup.shape
    cols = block.shape[1]
    group = lax.axis_size("leafin")
    me = lax.axis_index("leafin")
    index = jnp.arange(width, dtype=jnp.int32)
    mask = (index < mode_counts[0]).astype(F32)
    scaled = (coup.astype(F32) * (mask / eigenvalues[0])[None, :]).astype(BF16)

    coup_all = gather_direct(coup, "panel")
    rl = modal.shape[1] // group
    coup_all, coords = lax.optimization_barrier((coup_all, coords))
    scaled_late, modal_late = scaled, modal
    schur = block - lax.dot_general(scaled, coup_all, (((1,), (1,)), ((), ())), preferred_element_type=F32)
    modal3 = modal_late.reshape(modal.shape[0], group, rl)
    lhs, rhs = [scaled_late], [lax.dynamic_index_in_dim(modal3, me, 1, keepdims=False)]
    for d in range(1, group):
        lhs.append(swap(scaled_late, "leafin", d))
        rhs.append(swap(lax.dynamic_index_in_dim(modal3, me ^ d, 1, keepdims=False), "leafin", d))

    half = rows // 2
    piece = half // group
    merged = []
    for h in range(2):
        part = schur[h * half:(h + 1) * half].reshape(2, 2, piece, cols)
        summed = reduce_scatter_2d(part, h)
        merged.append(unpack(all_gather_2d(summed, h)).reshape(half, cols))
    merged = jnp.concatenate(merged, axis=0)

    modal_term = jnp.dot(jnp.concatenate(lhs, axis=1), jnp.concatenate(rhs, axis=0), preferred_element_type=F32)

    coords_all = gather_bits(coords, "panel")
    top = lax.reduce_precision(merged, exponent_bits=8, mantissa_bits=7)
    hi, lo = top.astype(BF16), (merged - top).astype(BF16)
    product = jnp.dot(lo, coords_all, preferred_element_type=F32) + jnp.dot(hi, coords_all, preferred_element_type=F32)
    return (modal_term + product)[None]


def solution(mesh):
    def run(*args):
        group = args[5].shape[2] // args[4].shape[2]
        leaves, panels = mesh.shape["leaf"], mesh.shape["panel"]
        grid = mesh.devices.reshape(leaves // group, group, panels)
        sub = Mesh(grid, ("grp", "leafin", "panel"))
        leaf = ("grp", "leafin")
        placed = (
            P(leaf, "panel", None),
            P(leaf, "panel", None),
            P(leaf, None),
            P(leaf),
            P(leaf, "panel", None),
            P(leaf, None, None),
        )
        body = jax.shard_map(on_device, mesh=sub, in_specs=placed, out_specs=P(leaf, "panel", None), check_vma=False)
        return body(*args)

    return run
```

```python
import jax
import jax.numpy as jnp
from jax import lax
from jax.sharding import Mesh, PartitionSpec as P

F32, BF16, F16 = jnp.float32, jnp.bfloat16, jnp.float16
TAG = 128


def swap(value, axis, mask):
    return lax.ppermute(value, axis, [(i, i ^ mask) for i in range(lax.axis_size(axis))])


def bit_of(axis, bit):
    return (lax.axis_index(axis) >> bit) & 1


def halves(stack, bit, axis=0):
    keep = lax.dynamic_index_in_dim(stack, bit, axis, keepdims=False)
    send = lax.dynamic_index_in_dim(stack, 1 - bit, axis, keepdims=False)
    return keep, send


def place(mine, other, bit, axis=0):
    return jnp.where(bit == 0, jnp.stack([mine, other], axis), jnp.stack([other, mine], axis))


def gather_direct(value, axis):
    size = lax.axis_size(axis)
    me = lax.axis_index(axis)
    rel = jnp.stack([value] + [swap(value, axis, d) for d in range(1, size)])
    return jnp.concatenate([lax.dynamic_index_in_dim(rel, q ^ me, 0, keepdims=False) for q in range(size)], 0)


def gather_bits(value, axis):
    bits = (lax.axis_size(axis) - 1).bit_length()
    out = value[None]
    for level, bit in enumerate(range(bits - 1, -1, -1)):
        other = swap(out, axis, 1 << bit)
        out = place(out, other, bit_of(axis, bit), axis=level)
    return out.reshape((-1,) + value.shape[1:])


def pack(x):
    top = jnp.max(jnp.abs(x), axis=-1, keepdims=True)
    shift = jnp.clip(jnp.floor(jnp.log2(jnp.maximum(top, 1e-30))), -100.0, 100.0)
    values = (x * jnp.exp2(-shift)).astype(F16)
    return jnp.concatenate([values, jnp.broadcast_to(shift, x.shape[:-1] + (TAG,)).astype(F16)], axis=-1)


def unpack(p):
    cols = p.shape[-1] - TAG
    return p[..., :cols].astype(F32) * jnp.exp2(p[..., cols:cols + 1].astype(F32))


def reduce_scatter_first(x, first):
    keep, send = halves(x, bit_of("leafin", first), axis=1 - first)
    return keep, swap(pack(send), "leafin", 1 << first)


def reduce_scatter_second(keep, got, first):
    second = 1 - first
    acc = keep + unpack(got)
    keep, send = halves(acc, bit_of("leafin", second), axis=0)
    return keep + unpack(swap(pack(send), "leafin", 1 << second))


def all_gather_2d(piece, first):
    last = 1 - first
    piece = pack(piece)
    got = place(piece, swap(piece, "leafin", 1 << last), bit_of("leafin", last))
    return place(got, swap(got, "leafin", 1 << first), bit_of("leafin", first), axis=1 - first)


def on_device(interface_block, coupling, eigenvalues, mode_counts, interface_coords, modal_coords):
    block = interface_block[0]
    coup = coupling[0]
    coords = interface_coords[0]
    modal = modal_coords[0]
    rows, width = coup.shape
    cols = block.shape[1]
    group = lax.axis_size("leafin")
    me = lax.axis_index("leafin")
    index = jnp.arange(width, dtype=jnp.int32)
    mask = (index < mode_counts[0]).astype(F32)
    scaled = (coup.astype(F32) * (mask / eigenvalues[0])[None, :]).astype(BF16)

    coup_all = gather_direct(coup, "panel")
    rl = modal.shape[1] // group
    coup_all, coords = lax.optimization_barrier((coup_all, coords))
    schur = block - lax.dot_general(scaled, coup_all, (((1,), (1,)), ((), ())), preferred_element_type=F32)
    half = rows // 2
    piece = half // group
    firsts = [reduce_scatter_first(schur[h * half:(h + 1) * half].reshape(2, 2, piece, cols), h) for h in range(2)]
    firsts, scaled_late, modal_late = lax.optimization_barrier((firsts, scaled, modal))
    modal3 = modal_late.reshape(modal.shape[0], group, rl)
    lhs, rhs = [scaled_late], [lax.dynamic_index_in_dim(modal3, me, 1, keepdims=False)]
    for d in range(1, group):
        lhs.append(swap(scaled_late, "leafin", d))
        rhs.append(swap(lax.dynamic_index_in_dim(modal3, me ^ d, 1, keepdims=False), "leafin", d))

    merged = []
    for h in range(2):
        summed = reduce_scatter_second(*firsts[h], h)
        merged.append(unpack(all_gather_2d(summed, h)).reshape(half, cols))
    merged = jnp.concatenate(merged, axis=0)

    modal_term = jnp.dot(jnp.concatenate(lhs, axis=1), jnp.concatenate(rhs, axis=0), preferred_element_type=F32)

    coords_all = gather_bits(coords, "panel")
    top = lax.reduce_precision(merged, exponent_bits=8, mantissa_bits=7)
    hi, lo = top.astype(BF16), (merged - top).astype(BF16)
    product = jnp.dot(lo, coords_all, preferred_element_type=F32) + jnp.dot(hi, coords_all, preferred_element_type=F32)
    return (modal_term + product)[None]


def solution(mesh):
    def run(*args):
        group = args[5].shape[2] // args[4].shape[2]
        leaves, panels = mesh.shape["leaf"], mesh.shape["panel"]
        grid = mesh.devices.reshape(leaves // group, group, panels)
        sub = Mesh(grid, ("grp", "leafin", "panel"))
        leaf = ("grp", "leafin")
        placed = (
            P(leaf, "panel", None),
            P(leaf, "panel", None),
            P(leaf, None),
            P(leaf),
            P(leaf, "panel", None),
            P(leaf, None, None),
        )
        body = jax.shard_map(on_device, mesh=sub, in_specs=placed, out_specs=P(leaf, "panel", None), check_vma=False)
        return body(*args)

    return run
```

```python
import jax
import jax.numpy as jnp
from jax import lax
from jax.sharding import Mesh, PartitionSpec as P

F32, BF16, F16 = jnp.float32, jnp.bfloat16, jnp.float16
TAG = 128


def swap(value, axis, mask):
    return lax.ppermute(value, axis, [(i, i ^ mask) for i in range(lax.axis_size(axis))])


def bit_of(axis, bit):
    return (lax.axis_index(axis) >> bit) & 1


def halves(stack, bit, axis=0):
    keep = lax.dynamic_index_in_dim(stack, bit, axis, keepdims=False)
    send = lax.dynamic_index_in_dim(stack, 1 - bit, axis, keepdims=False)
    return keep, send


def place(mine, other, bit, axis=0):
    return jnp.where(bit == 0, jnp.stack([mine, other], axis), jnp.stack([other, mine], axis))


def gather_direct(value, axis):
    size = lax.axis_size(axis)
    me = lax.axis_index(axis)
    rel = jnp.stack([value] + [swap(value, axis, d) for d in range(1, size)])
    return jnp.concatenate([lax.dynamic_index_in_dim(rel, q ^ me, 0, keepdims=False) for q in range(size)], 0)


def gather_bits(value, axis):
    bits = (lax.axis_size(axis) - 1).bit_length()
    out = value[None]
    for level, bit in enumerate(range(bits - 1, -1, -1)):
        other = swap(out, axis, 1 << bit)
        out = place(out, other, bit_of(axis, bit), axis=level)
    return out.reshape((-1,) + value.shape[1:])


def pack(x):
    top = jnp.max(jnp.abs(x), axis=-1, keepdims=True)
    shift = jnp.clip(jnp.floor(jnp.log2(jnp.maximum(top, 1e-30))), -100.0, 100.0)
    values = (x * jnp.exp2(-shift)).astype(F16)
    return jnp.concatenate([values, jnp.broadcast_to(shift, x.shape[:-1] + (TAG,)).astype(F16)], axis=-1)


def unpack(p):
    cols = p.shape[-1] - TAG
    return p[..., :cols].astype(F32) * jnp.exp2(p[..., cols:cols + 1].astype(F32))


def reduce_scatter_2d(x, first):
    second = 1 - first
    keep, send = halves(x, bit_of("leafin", first), axis=1 - first)
    acc = keep + unpack(swap(pack(send), "leafin", 1 << first))
    keep, send = halves(acc, bit_of("leafin", second), axis=0)
    return keep + unpack(swap(pack(send), "leafin", 1 << second))


def all_gather_2d(piece, first):
    last = 1 - first
    piece = pack(piece)
    got = place(piece, swap(piece, "leafin", 1 << last), bit_of("leafin", last))
    return place(got, swap(got, "leafin", 1 << first), bit_of("leafin", first), axis=1 - first)


def on_device(interface_block, coupling, eigenvalues, mode_counts, interface_coords, modal_coords):
    block = interface_block[0]
    coup = coupling[0]
    coords = interface_coords[0]
    modal = modal_coords[0]
    rows, width = coup.shape
    cols = block.shape[1]
    group = lax.axis_size("leafin")
    me = lax.axis_index("leafin")
    index = jnp.arange(width, dtype=jnp.int32)
    mask = (index < mode_counts[0]).astype(F32)
    scaled = (coup.astype(F32) * (mask / eigenvalues[0])[None, :]).astype(BF16)

    coup_all = gather_direct(coup, "panel")
    rl = modal.shape[1] // group
    coup_all, coords = lax.optimization_barrier((coup_all, coords))
    scaled_late, modal_late = scaled, modal
    schur = block - lax.dot_general(scaled, coup_all, (((1,), (1,)), ((), ())), preferred_element_type=F32)
    modal3 = modal_late.reshape(modal.shape[0], group, rl)
    lhs, rhs = [scaled_late], [lax.dynamic_index_in_dim(modal3, me, 1, keepdims=False)]
    for d in range(1, group):
        lhs.append(swap(scaled_late, "leafin", d))
        rhs.append(swap(lax.dynamic_index_in_dim(modal3, me ^ d, 1, keepdims=False), "leafin", d))

    half = rows // 2
    piece = half // group
    summed = [reduce_scatter_2d(schur[h * half:(h + 1) * half].reshape(2, 2, piece, cols), h) for h in range(2)]
    modal_term = jnp.dot(jnp.concatenate(lhs, axis=1), jnp.concatenate(rhs, axis=0), preferred_element_type=F32)
    summed, modal_term = lax.optimization_barrier((summed, modal_term))
    merged = jnp.concatenate([unpack(all_gather_2d(summed[h], h)).reshape(half, cols) for h in range(2)], axis=0)

    coords_all = gather_bits(coords, "panel")
    top = lax.reduce_precision(merged, exponent_bits=8, mantissa_bits=7)
    hi, lo = top.astype(BF16), (merged - top).astype(BF16)
    product = jnp.dot(lo, coords_all, preferred_element_type=F32) + jnp.dot(hi, coords_all, preferred_element_type=F32)
    return (modal_term + product)[None]


def solution(mesh):
    def run(*args):
        group = args[5].shape[2] // args[4].shape[2]
        leaves, panels = mesh.shape["leaf"], mesh.shape["panel"]
        grid = mesh.devices.reshape(leaves // group, group, panels)
        sub = Mesh(grid, ("grp", "leafin", "panel"))
        leaf = ("grp", "leafin")
        placed = (
            P(leaf, "panel", None),
            P(leaf, "panel", None),
            P(leaf, None),
            P(leaf),
            P(leaf, "panel", None),
            P(leaf, None, None),
        )
        body = jax.shard_map(on_device, mesh=sub, in_specs=placed, out_specs=P(leaf, "panel", None), check_vma=False)
        return body(*args)

    return run
```

```python
import jax
import jax.numpy as jnp
from jax import lax
from jax.sharding import Mesh, PartitionSpec as P

F32, BF16, F16 = jnp.float32, jnp.bfloat16, jnp.float16
TAG = 128


def swap(value, axis, mask):
    return lax.ppermute(value, axis, [(i, i ^ mask) for i in range(lax.axis_size(axis))])


def bit_of(axis, bit):
    return (lax.axis_index(axis) >> bit) & 1


def halves(stack, bit, axis=0):
    keep = lax.dynamic_index_in_dim(stack, bit, axis, keepdims=False)
    send = lax.dynamic_index_in_dim(stack, 1 - bit, axis, keepdims=False)
    return keep, send


def place(mine, other, bit, axis=0):
    return jnp.where(bit == 0, jnp.stack([mine, other], axis), jnp.stack([other, mine], axis))


def gather_direct(value, axis):
    size = lax.axis_size(axis)
    me = lax.axis_index(axis)
    rel = jnp.stack([value] + [swap(value, axis, d) for d in range(1, size)])
    return jnp.concatenate([lax.dynamic_index_in_dim(rel, q ^ me, 0, keepdims=False) for q in range(size)], 0)


def gather_bits(value, axis):
    bits = (lax.axis_size(axis) - 1).bit_length()
    out = value[None]
    for level, bit in enumerate(range(bits - 1, -1, -1)):
        other = swap(out, axis, 1 << bit)
        out = place(out, other, bit_of(axis, bit), axis=level)
    return out.reshape((-1,) + value.shape[1:])


def pack(x):
    top = jnp.max(jnp.abs(x), axis=-1, keepdims=True)
    shift = jnp.clip(jnp.floor(jnp.log2(jnp.maximum(top, 1e-30))), -100.0, 100.0)
    values = (x * jnp.exp2(-shift)).astype(F16)
    return jnp.concatenate([values, jnp.broadcast_to(shift, x.shape[:-1] + (TAG,)).astype(F16)], axis=-1)


def unpack(p):
    cols = p.shape[-1] - TAG
    return p[..., :cols].astype(F32) * jnp.exp2(p[..., cols:cols + 1].astype(F32))


def reduce_scatter_2d(x, first):
    second = 1 - first
    keep, send = halves(x, bit_of("leafin", first), axis=1 - first)
    acc = keep + unpack(swap(pack(send), "leafin", 1 << first))
    keep, send = halves(acc, bit_of("leafin", second), axis=0)
    return keep + unpack(swap(pack(send), "leafin", 1 << second))


def all_gather_2d(piece, first):
    last = 1 - first
    piece = pack(piece)
    got = place(piece, swap(piece, "leafin", 1 << last), bit_of("leafin", last))
    return place(got, swap(got, "leafin", 1 << first), bit_of("leafin", first), axis=1 - first)


def on_device(interface_block, coupling, eigenvalues, mode_counts, interface_coords, modal_coords):
    block = interface_block[0]
    coup = coupling[0]
    coords = interface_coords[0]
    modal = modal_coords[0]
    rows, width = coup.shape
    cols = block.shape[1]
    group = lax.axis_size("leafin")
    me = lax.axis_index("leafin")
    index = jnp.arange(width, dtype=jnp.int32)
    mask = (index < mode_counts[0]).astype(F32)
    scaled = (coup.astype(F32) * (mask / eigenvalues[0])[None, :]).astype(BF16)

    coup_all = gather_direct(coup, "panel")
    rl = modal.shape[1] // group
    scaled_late, modal_late = scaled, modal
    schur = block - lax.dot_general(scaled, coup_all, (((1,), (1,)), ((), ())), preferred_element_type=F32)
    modal3 = modal_late.reshape(modal.shape[0], group, rl)
    lhs, rhs = [scaled_late], [lax.dynamic_index_in_dim(modal3, me, 1, keepdims=False)]
    for d in range(1, group):
        lhs.append(swap(scaled_late, "leafin", d))
        rhs.append(swap(lax.dynamic_index_in_dim(modal3, me ^ d, 1, keepdims=False), "leafin", d))

    half = rows // 2
    piece = half // group
    merged = []
    for h in range(2):
        part = schur[h * half:(h + 1) * half].reshape(2, 2, piece, cols)
        summed = reduce_scatter_2d(part, h)
        merged.append(unpack(all_gather_2d(summed, h)).reshape(half, cols))
    merged = jnp.concatenate(merged, axis=0)

    modal_term = jnp.dot(jnp.concatenate(lhs, axis=1), jnp.concatenate(rhs, axis=0), preferred_element_type=F32)

    coords_all = gather_bits(coords, "panel")
    top = lax.reduce_precision(merged, exponent_bits=8, mantissa_bits=7)
    hi, lo = top.astype(BF16), (merged - top).astype(BF16)
    product = jnp.dot(lo, coords_all, preferred_element_type=F32) + jnp.dot(hi, coords_all, preferred_element_type=F32)
    return (modal_term + product)[None]


def solution(mesh):
    def run(*args):
        group = args[5].shape[2] // args[4].shape[2]
        leaves, panels = mesh.shape["leaf"], mesh.shape["panel"]
        grid = mesh.devices.reshape(leaves // group, group, panels)
        sub = Mesh(grid, ("grp", "leafin", "panel"))
        leaf = ("grp", "leafin")
        placed = (
            P(leaf, "panel", None),
            P(leaf, "panel", None),
            P(leaf, None),
            P(leaf),
            P(leaf, "panel", None),
            P(leaf, None, None),
        )
        body = jax.shard_map(on_device, mesh=sub, in_specs=placed, out_specs=P(leaf, "panel", None), check_vma=False)
        return body(*args)

    return run
```

```python
import jax
import jax.numpy as jnp
from jax import lax
from jax.sharding import Mesh, PartitionSpec as P

F32, BF16, F16 = jnp.float32, jnp.bfloat16, jnp.float16
TAG = 128


def swap(value, axis, mask):
    return lax.ppermute(value, axis, [(i, i ^ mask) for i in range(lax.axis_size(axis))])


def bit_of(axis, bit):
    return (lax.axis_index(axis) >> bit) & 1


def halves(stack, bit, axis=0):
    keep = lax.dynamic_index_in_dim(stack, bit, axis, keepdims=False)
    send = lax.dynamic_index_in_dim(stack, 1 - bit, axis, keepdims=False)
    return keep, send


def place(mine, other, bit, axis=0):
    return jnp.where(bit == 0, jnp.stack([mine, other], axis), jnp.stack([other, mine], axis))


def gather_direct(value, axis):
    size = lax.axis_size(axis)
    me = lax.axis_index(axis)
    rel = jnp.stack([value] + [swap(value, axis, d) for d in range(1, size)])
    return jnp.concatenate([lax.dynamic_index_in_dim(rel, q ^ me, 0, keepdims=False) for q in range(size)], 0)


def gather_bits(value, axis):
    bits = (lax.axis_size(axis) - 1).bit_length()
    out = value[None]
    for level, bit in enumerate(range(bits - 1, -1, -1)):
        other = swap(out, axis, 1 << bit)
        out = place(out, other, bit_of(axis, bit), axis=level)
    return out.reshape((-1,) + value.shape[1:])


def pack(x):
    top = jnp.max(jnp.abs(x), axis=-1, keepdims=True)
    shift = jnp.clip(jnp.floor(jnp.log2(jnp.maximum(top, 1e-30))), -100.0, 100.0)
    values = (x * jnp.exp2(-shift)).astype(F16)
    return jnp.concatenate([values, jnp.broadcast_to(shift, x.shape[:-1] + (TAG,)).astype(F16)], axis=-1)


def unpack(p):
    cols = p.shape[-1] - TAG
    return p[..., :cols].astype(F32) * jnp.exp2(p[..., cols:cols + 1].astype(F32))


def reduce_scatter_pack(x, first):
    keep, send = halves(x, bit_of("leafin", first), axis=1 - first)
    return keep, pack(send)


def reduce_scatter_rest(keep, packed, first):
    second = 1 - first
    acc = keep + unpack(swap(packed, "leafin", 1 << first))
    keep, send = halves(acc, bit_of("leafin", second), axis=0)
    return keep + unpack(swap(pack(send), "leafin", 1 << second))


def all_gather_2d(piece, first):
    last = 1 - first
    piece = pack(piece)
    got = place(piece, swap(piece, "leafin", 1 << last), bit_of("leafin", last))
    return place(got, swap(got, "leafin", 1 << first), bit_of("leafin", first), axis=1 - first)


def on_device(interface_block, coupling, eigenvalues, mode_counts, interface_coords, modal_coords):
    block = interface_block[0]
    coup = coupling[0]
    coords = interface_coords[0]
    modal = modal_coords[0]
    rows, width = coup.shape
    cols = block.shape[1]
    group = lax.axis_size("leafin")
    me = lax.axis_index("leafin")
    index = jnp.arange(width, dtype=jnp.int32)
    mask = (index < mode_counts[0]).astype(F32)
    scaled = (coup.astype(F32) * (mask / eigenvalues[0])[None, :]).astype(BF16)

    coup_all = gather_direct(coup, "panel")
    rl = modal.shape[1] // group
    schur = block - lax.dot_general(scaled, coup_all, (((1,), (1,)), ((), ())), preferred_element_type=F32)
    half = rows // 2
    piece = half // group
    firsts = [reduce_scatter_pack(schur[h * half:(h + 1) * half].reshape(2, 2, piece, cols), h) for h in range(2)]
    firsts, scaled_late, modal_late = lax.optimization_barrier((firsts, scaled, modal))
    summed = [reduce_scatter_rest(*firsts[h], h) for h in range(2)]
    modal3 = modal_late.reshape(modal.shape[0], group, rl)
    lhs, rhs = [scaled_late], [lax.dynamic_index_in_dim(modal3, me, 1, keepdims=False)]
    for d in range(1, group):
        lhs.append(swap(scaled_late, "leafin", d))
        rhs.append(swap(lax.dynamic_index_in_dim(modal3, me ^ d, 1, keepdims=False), "leafin", d))
    merged = jnp.concatenate([unpack(all_gather_2d(summed[h], h)).reshape(half, cols) for h in range(2)], axis=0)

    modal_term = jnp.dot(jnp.concatenate(lhs, axis=1), jnp.concatenate(rhs, axis=0), preferred_element_type=F32)

    coords_all = gather_bits(coords, "panel")
    top = lax.reduce_precision(merged, exponent_bits=8, mantissa_bits=7)
    hi, lo = top.astype(BF16), (merged - top).astype(BF16)
    product = jnp.dot(lo, coords_all, preferred_element_type=F32) + jnp.dot(hi, coords_all, preferred_element_type=F32)
    return (modal_term + product)[None]


def solution(mesh):
    def run(*args):
        group = args[5].shape[2] // args[4].shape[2]
        leaves, panels = mesh.shape["leaf"], mesh.shape["panel"]
        grid = mesh.devices.reshape(leaves // group, group, panels)
        sub = Mesh(grid, ("grp", "leafin", "panel"))
        leaf = ("grp", "leafin")
        placed = (
            P(leaf, "panel", None),
            P(leaf, "panel", None),
            P(leaf, None),
            P(leaf),
            P(leaf, "panel", None),
            P(leaf, None, None),
        )
        body = jax.shard_map(on_device, mesh=sub, in_specs=placed, out_specs=P(leaf, "panel", None), check_vma=False)
        return body(*args)

    return run
```

```python
import jax
import jax.numpy as jnp
from jax import lax
from jax.sharding import Mesh, PartitionSpec as P

F32, BF16, F16 = jnp.float32, jnp.bfloat16, jnp.float16
TAG = 128


def swap(value, axis, mask):
    return lax.ppermute(value, axis, [(i, i ^ mask) for i in range(lax.axis_size(axis))])


def bit_of(axis, bit):
    return (lax.axis_index(axis) >> bit) & 1


def halves(stack, bit, axis=0):
    keep = lax.dynamic_index_in_dim(stack, bit, axis, keepdims=False)
    send = lax.dynamic_index_in_dim(stack, 1 - bit, axis, keepdims=False)
    return keep, send


def place(mine, other, bit, axis=0):
    return jnp.where(bit == 0, jnp.stack([mine, other], axis), jnp.stack([other, mine], axis))


def gather_direct(value, axis):
    size = lax.axis_size(axis)
    me = lax.axis_index(axis)
    rel = jnp.stack([value] + [swap(value, axis, d) for d in range(1, size)])
    return jnp.concatenate([lax.dynamic_index_in_dim(rel, q ^ me, 0, keepdims=False) for q in range(size)], 0)


def gather_bits(value, axis):
    bits = (lax.axis_size(axis) - 1).bit_length()
    out = value[None]
    for level, bit in enumerate(range(bits - 1, -1, -1)):
        other = swap(out, axis, 1 << bit)
        out = place(out, other, bit_of(axis, bit), axis=level)
    return out.reshape((-1,) + value.shape[1:])


def pack(x):
    top = jnp.max(jnp.abs(x), axis=-1, keepdims=True)
    shift = jnp.clip(jnp.floor(jnp.log2(jnp.maximum(top, 1e-30))), -100.0, 100.0)
    values = (x * jnp.exp2(-shift)).astype(F16)
    return jnp.concatenate([values, jnp.broadcast_to(shift, x.shape[:-1] + (TAG,)).astype(F16)], axis=-1)


def unpack(p):
    cols = p.shape[-1] - TAG
    return p[..., :cols].astype(F32) * jnp.exp2(p[..., cols:cols + 1].astype(F32))


def reduce_scatter_2d(x, first):
    second = 1 - first
    keep, send = halves(x, bit_of("leafin", first), axis=1 - first)
    acc = keep + unpack(swap(pack(send), "leafin", 1 << first))
    keep, send = halves(acc, bit_of("leafin", second), axis=0)
    return keep + unpack(swap(pack(send), "leafin", 1 << second))


def all_gather_2d(piece, first):
    last = 1 - first
    piece = pack(piece)
    got = place(piece, swap(piece, "leafin", 1 << last), bit_of("leafin", last))
    return place(got, swap(got, "leafin", 1 << first), bit_of("leafin", first), axis=1 - first)


def on_device(interface_block, coupling, eigenvalues, mode_counts, interface_coords, modal_coords):
    block = interface_block[0]
    coup = coupling[0]
    coords = interface_coords[0]
    modal = modal_coords[0]
    rows, width = coup.shape
    cols = block.shape[1]
    group = lax.axis_size("leafin")
    me = lax.axis_index("leafin")
    index = jnp.arange(width, dtype=jnp.int32)
    mask = (index < mode_counts[0]).astype(F32)
    scaled = (coup.astype(F32) * (mask / eigenvalues[0])[None, :]).astype(BF16)

    coup_all = gather_direct(coup, "panel")
    rl = modal.shape[1] // group
    scaled_late, modal_late = scaled, modal
    schur = block - lax.dot_general(scaled, coup_all, (((1,), (1,)), ((), ())), preferred_element_type=F32)
    modal3 = modal_late.reshape(modal.shape[0], group, rl)
    own_part = lax.dynamic_index_in_dim(modal3, me, 1, keepdims=False)
    lhs, rhs = [scaled_late], [own_part]
    for d in range(1, group):
        part = lax.dynamic_index_in_dim(modal3, me ^ d, 1, keepdims=False).reshape(-1, width)
        got = swap(jnp.concatenate([scaled_late, part], axis=0), "leafin", d)
        lhs.append(got[:rows])
        rhs.append(got[rows:].reshape(own_part.shape))

    half = rows // 2
    piece = half // group
    merged = []
    for h in range(2):
        part = schur[h * half:(h + 1) * half].reshape(2, 2, piece, cols)
        summed = reduce_scatter_2d(part, h)
        merged.append(unpack(all_gather_2d(summed, h)).reshape(half, cols))
    merged = jnp.concatenate(merged, axis=0)

    modal_term = jnp.dot(jnp.concatenate(lhs, axis=1), jnp.concatenate(rhs, axis=0), preferred_element_type=F32)

    coords_all = gather_bits(coords, "panel")
    top = lax.reduce_precision(merged, exponent_bits=8, mantissa_bits=7)
    hi, lo = top.astype(BF16), (merged - top).astype(BF16)
    product = jnp.dot(lo, coords_all, preferred_element_type=F32) + jnp.dot(hi, coords_all, preferred_element_type=F32)
    return (modal_term + product)[None]


def solution(mesh):
    def run(*args):
        group = args[5].shape[2] // args[4].shape[2]
        leaves, panels = mesh.shape["leaf"], mesh.shape["panel"]
        grid = mesh.devices.reshape(leaves // group, group, panels)
        sub = Mesh(grid, ("grp", "leafin", "panel"))
        leaf = ("grp", "leafin")
        placed = (
            P(leaf, "panel", None),
            P(leaf, "panel", None),
            P(leaf, None),
            P(leaf),
            P(leaf, "panel", None),
            P(leaf, None, None),
        )
        body = jax.shard_map(on_device, mesh=sub, in_specs=placed, out_specs=P(leaf, "panel", None), check_vma=False)
        return body(*args)

    return run
```

```python
import jax
import jax.numpy as jnp
from jax import lax
from jax.sharding import Mesh, PartitionSpec as P

F32, BF16, F16 = jnp.float32, jnp.bfloat16, jnp.float16
TAG = 128


def swap(value, axis, mask):
    return lax.ppermute(value, axis, [(i, i ^ mask) for i in range(lax.axis_size(axis))])


def bit_of(axis, bit):
    return (lax.axis_index(axis) >> bit) & 1


def halves(stack, bit, axis=0):
    keep = lax.dynamic_index_in_dim(stack, bit, axis, keepdims=False)
    send = lax.dynamic_index_in_dim(stack, 1 - bit, axis, keepdims=False)
    return keep, send


def place(mine, other, bit, axis=0):
    return jnp.where(bit == 0, jnp.stack([mine, other], axis), jnp.stack([other, mine], axis))


def gather_direct(value, axis):
    size = lax.axis_size(axis)
    me = lax.axis_index(axis)
    rel = jnp.stack([value] + [swap(value, axis, d) for d in range(1, size)])
    return jnp.concatenate([lax.dynamic_index_in_dim(rel, q ^ me, 0, keepdims=False) for q in range(size)], 0)


def gather_forward(value, axis):
    size = lax.axis_size(axis)
    held = {0: value}
    for bit in range((size - 1).bit_length() - 1, -1, -1):
        held.update({r | 1 << bit: swap(v, axis, 1 << bit) for r, v in list(held.items())})
    rel = jnp.stack([held[r] for r in range(size)])
    me = lax.axis_index(axis)
    return jnp.concatenate([lax.dynamic_index_in_dim(rel, q ^ me, 0, keepdims=False) for q in range(size)], 0)


def gather_bits(value, axis):
    bits = (lax.axis_size(axis) - 1).bit_length()
    out = value[None]
    for level, bit in enumerate(range(bits - 1, -1, -1)):
        other = swap(out, axis, 1 << bit)
        out = place(out, other, bit_of(axis, bit), axis=level)
    return out.reshape((-1,) + value.shape[1:])


def pack(x):
    top = jnp.max(jnp.abs(x), axis=-1, keepdims=True)
    shift = jnp.clip(jnp.floor(jnp.log2(jnp.maximum(top, 1e-30))), -100.0, 100.0)
    values = (x * jnp.exp2(-shift)).astype(F16)
    return jnp.concatenate([values, jnp.broadcast_to(shift, x.shape[:-1] + (TAG,)).astype(F16)], axis=-1)


def unpack(p):
    cols = p.shape[-1] - TAG
    return p[..., :cols].astype(F32) * jnp.exp2(p[..., cols:cols + 1].astype(F32))


def reduce_scatter_2d(x, first):
    second = 1 - first
    keep, send = halves(x, bit_of("leafin", first), axis=1 - first)
    acc = keep + unpack(swap(pack(send), "leafin", 1 << first))
    keep, send = halves(acc, bit_of("leafin", second), axis=0)
    return keep + unpack(swap(pack(send), "leafin", 1 << second))


def all_gather_2d(piece, first):
    last = 1 - first
    piece = pack(piece)
    got = place(piece, swap(piece, "leafin", 1 << last), bit_of("leafin", last))
    return place(got, swap(got, "leafin", 1 << first), bit_of("leafin", first), axis=1 - first)


def on_device(interface_block, coupling, eigenvalues, mode_counts, interface_coords, modal_coords):
    block = interface_block[0]
    coup = coupling[0]
    coords = interface_coords[0]
    modal = modal_coords[0]
    rows, width = coup.shape
    cols = block.shape[1]
    group = lax.axis_size("leafin")
    me = lax.axis_index("leafin")
    index = jnp.arange(width, dtype=jnp.int32)
    mask = (index < mode_counts[0]).astype(F32)
    scaled = (coup.astype(F32) * (mask / eigenvalues[0])[None, :]).astype(BF16)

    coup_all = gather_direct(coup, "panel")
    rl = modal.shape[1] // group
    scaled_late, modal_late = scaled, modal
    schur = block - lax.dot_general(scaled, coup_all, (((1,), (1,)), ((), ())), preferred_element_type=F32)
    modal3 = modal_late.reshape(modal.shape[0], group, rl)
    lhs, rhs = [scaled_late], [lax.dynamic_index_in_dim(modal3, me, 1, keepdims=False)]
    for d in range(1, group):
        lhs.append(swap(scaled_late, "leafin", d))
        rhs.append(swap(lax.dynamic_index_in_dim(modal3, me ^ d, 1, keepdims=False), "leafin", d))

    half = rows // 2
    piece = half // group
    merged = []
    for h in range(2):
        part = schur[h * half:(h + 1) * half].reshape(2, 2, piece, cols)
        summed = reduce_scatter_2d(part, h)
        merged.append(unpack(all_gather_2d(summed, h)).reshape(half, cols))
    merged = jnp.concatenate(merged, axis=0)

    modal_term = jnp.dot(jnp.concatenate(lhs, axis=1), jnp.concatenate(rhs, axis=0), preferred_element_type=F32)

    coords_all = gather_forward(coords, "panel")
    top = lax.reduce_precision(merged, exponent_bits=8, mantissa_bits=7)
    hi, lo = top.astype(BF16), (merged - top).astype(BF16)
    product = jnp.dot(lo, coords_all, preferred_element_type=F32) + jnp.dot(hi, coords_all, preferred_element_type=F32)
    return (modal_term + product)[None]


def solution(mesh):
    def run(*args):
        group = args[5].shape[2] // args[4].shape[2]
        leaves, panels = mesh.shape["leaf"], mesh.shape["panel"]
        grid = mesh.devices.reshape(leaves // group, group, panels)
        sub = Mesh(grid, ("grp", "leafin", "panel"))
        leaf = ("grp", "leafin")
        placed = (
            P(leaf, "panel", None),
            P(leaf, "panel", None),
            P(leaf, None),
            P(leaf),
            P(leaf, "panel", None),
            P(leaf, None, None),
        )
        body = jax.shard_map(on_device, mesh=sub, in_specs=placed, out_specs=P(leaf, "panel", None), check_vma=False)
        return body(*args)

    return run
```

```python
import jax
import jax.numpy as jnp
from jax import lax
from jax.sharding import Mesh, PartitionSpec as P

F32, BF16, F16 = jnp.float32, jnp.bfloat16, jnp.float16
TAG = 128


def swap(value, axis, mask):
    return lax.ppermute(value, axis, [(i, i ^ mask) for i in range(lax.axis_size(axis))])


def bit_of(axis, bit):
    return (lax.axis_index(axis) >> bit) & 1


def halves(stack, bit, axis=0):
    keep = lax.dynamic_index_in_dim(stack, bit, axis, keepdims=False)
    send = lax.dynamic_index_in_dim(stack, 1 - bit, axis, keepdims=False)
    return keep, send


def place(mine, other, bit, axis=0):
    return jnp.where(bit == 0, jnp.stack([mine, other], axis), jnp.stack([other, mine], axis))


def gather_direct(value, axis):
    size = lax.axis_size(axis)
    me = lax.axis_index(axis)
    rel = jnp.stack([value] + [swap(value, axis, d) for d in range(1, size)])
    return jnp.concatenate([lax.dynamic_index_in_dim(rel, q ^ me, 0, keepdims=False) for q in range(size)], 0)


def gather_bits(value, axis):
    bits = (lax.axis_size(axis) - 1).bit_length()
    out = value[None]
    for level, bit in enumerate(range(bits - 1, -1, -1)):
        other = swap(out, axis, 1 << bit)
        out = place(out, other, bit_of(axis, bit), axis=level)
    return out.reshape((-1,) + value.shape[1:])


def pack(x):
    top = jnp.max(jnp.abs(x), axis=-1, keepdims=True)
    shift = jnp.clip(jnp.floor(jnp.log2(jnp.maximum(top, 1e-30))), -100.0, 100.0)
    values = (x * jnp.exp2(-shift)).astype(F16)
    return jnp.concatenate([values, jnp.broadcast_to(shift, x.shape[:-1] + (TAG,)).astype(F16)], axis=-1)


def unpack(p):
    cols = p.shape[-1] - TAG
    return p[..., :cols].astype(F32) * jnp.exp2(p[..., cols:cols + 1].astype(F32))


def reduce_scatter_2d(x, first):
    second = 1 - first
    keep, send = halves(x, bit_of("leafin", first), axis=1 - first)
    acc = keep + unpack(swap(pack(send), "leafin", 1 << first))
    keep, send = halves(acc, bit_of("leafin", second), axis=0)
    return keep + unpack(swap(pack(send), "leafin", 1 << second))


def all_gather_2d(piece, first):
    last = 1 - first
    piece = pack(piece)
    got = place(piece, swap(piece, "leafin", 1 << last), bit_of("leafin", last))
    return place(got, swap(got, "leafin", 1 << first), bit_of("leafin", first), axis=1 - first)


def on_device(interface_block, coupling, eigenvalues, mode_counts, interface_coords, modal_coords):
    block = interface_block[0]
    coup = coupling[0]
    coords = interface_coords[0]
    modal = modal_coords[0]
    rows, width = coup.shape
    cols = block.shape[1]
    group = lax.axis_size("leafin")
    me = lax.axis_index("leafin")
    index = jnp.arange(width, dtype=jnp.int32)
    mask = (index < mode_counts[0]).astype(F32)
    scaled = (coup.astype(F32) * (mask / eigenvalues[0])[None, :]).astype(BF16)

    coup_all = gather_direct(coup, "panel")
    rl = modal.shape[1] // group
    coup_all, scaled_late, modal_late = lax.optimization_barrier((coup_all, scaled, modal))
    schur = block - lax.dot_general(scaled, coup_all, (((1,), (1,)), ((), ())), preferred_element_type=F32)
    modal3 = modal_late.reshape(modal.shape[0], group, rl)
    lhs, rhs = [scaled_late], [lax.dynamic_index_in_dim(modal3, me, 1, keepdims=False)]
    for d in range(1, group):
        lhs.append(swap(scaled_late, "leafin", d))
        rhs.append(swap(lax.dynamic_index_in_dim(modal3, me ^ d, 1, keepdims=False), "leafin", d))

    half = rows // 2
    piece = half // group
    merged = []
    for h in range(2):
        part = schur[h * half:(h + 1) * half].reshape(2, 2, piece, cols)
        summed = reduce_scatter_2d(part, h)
        merged.append(unpack(all_gather_2d(summed, h)).reshape(half, cols))
    merged = jnp.concatenate(merged, axis=0)

    modal_term = jnp.dot(jnp.concatenate(lhs, axis=1), jnp.concatenate(rhs, axis=0), preferred_element_type=F32)

    coords_all = gather_bits(coords, "panel")
    top = lax.reduce_precision(merged, exponent_bits=8, mantissa_bits=7)
    hi, lo = top.astype(BF16), (merged - top).astype(BF16)
    product = jnp.dot(lo, coords_all, preferred_element_type=F32) + jnp.dot(hi, coords_all, preferred_element_type=F32)
    return (modal_term + product)[None]


def solution(mesh):
    def run(*args):
        group = args[5].shape[2] // args[4].shape[2]
        leaves, panels = mesh.shape["leaf"], mesh.shape["panel"]
        grid = mesh.devices.reshape(leaves // group, group, panels)
        sub = Mesh(grid, ("grp", "leafin", "panel"))
        leaf = ("grp", "leafin")
        placed = (
            P(leaf, "panel", None),
            P(leaf, "panel", None),
            P(leaf, None),
            P(leaf),
            P(leaf, "panel", None),
            P(leaf, None, None),
        )
        body = jax.shard_map(on_device, mesh=sub, in_specs=placed, out_specs=P(leaf, "panel", None), check_vma=False)
        return body(*args)

    return run
```

```python
import jax
import jax.numpy as jnp
from jax import lax
from jax.sharding import Mesh, PartitionSpec as P

F32, BF16, F16 = jnp.float32, jnp.bfloat16, jnp.float16
TAG = 128


def swap(value, axis, mask):
    return lax.ppermute(value, axis, [(i, i ^ mask) for i in range(lax.axis_size(axis))])


def bit_of(axis, bit):
    return (lax.axis_index(axis) >> bit) & 1


def halves(stack, bit, axis=0):
    keep = lax.dynamic_index_in_dim(stack, bit, axis, keepdims=False)
    send = lax.dynamic_index_in_dim(stack, 1 - bit, axis, keepdims=False)
    return keep, send


def place(mine, other, bit, axis=0):
    return jnp.where(bit == 0, jnp.stack([mine, other], axis), jnp.stack([other, mine], axis))


def gather_direct(value, axis):
    size = lax.axis_size(axis)
    me = lax.axis_index(axis)
    rel = jnp.stack([value] + [swap(value, axis, d) for d in range(1, size)])
    return jnp.concatenate([lax.dynamic_index_in_dim(rel, q ^ me, 0, keepdims=False) for q in range(size)], 0)


def gather_bits(value, axis):
    bits = (lax.axis_size(axis) - 1).bit_length()
    out = value[None]
    for level, bit in enumerate(range(bits - 1, -1, -1)):
        other = swap(out, axis, 1 << bit)
        out = place(out, other, bit_of(axis, bit), axis=level)
    return out.reshape((-1,) + value.shape[1:])


def pack(x):
    top = jnp.max(jnp.abs(x), axis=-1, keepdims=True)
    shift = jnp.clip(jnp.floor(jnp.log2(jnp.maximum(top, 1e-30))), -100.0, 100.0)
    values = (x * jnp.exp2(-shift)).astype(F16)
    return jnp.concatenate([values, jnp.broadcast_to(shift, x.shape[:-1] + (TAG,)).astype(F16)], axis=-1)


def unpack(p):
    cols = p.shape[-1] - TAG
    return p[..., :cols].astype(F32) * jnp.exp2(p[..., cols:cols + 1].astype(F32))


def reduce_scatter_2d(x, first):
    second = 1 - first
    keep, send = halves(x, bit_of("leafin", first), axis=1 - first)
    acc = keep + unpack(swap(pack(send), "leafin", 1 << first))
    keep, send = halves(acc, bit_of("leafin", second), axis=0)
    return keep + unpack(swap(pack(send), "leafin", 1 << second))


def all_gather_2d(piece, first):
    last = 1 - first
    piece = pack(piece)
    got = place(piece, swap(piece, "leafin", 1 << last), bit_of("leafin", last))
    return place(got, swap(got, "leafin", 1 << first), bit_of("leafin", first), axis=1 - first)


def on_device(interface_block, coupling, eigenvalues, mode_counts, interface_coords, modal_coords):
    block = interface_block[0]
    coup = coupling[0]
    coords = interface_coords[0]
    modal = modal_coords[0]
    rows, width = coup.shape
    cols = block.shape[1]
    group = lax.axis_size("leafin")
    me = lax.axis_index("leafin")
    index = jnp.arange(width, dtype=jnp.int32)
    mask = (index < mode_counts[0]).astype(F32)
    scaled = (coup.astype(F32) * (mask / eigenvalues[0])[None, :]).astype(BF16)

    coup_all = gather_direct(coup, "panel")
    rl = modal.shape[1] // group
    scaled_late, modal_late = scaled, modal
    schur = block - lax.dot_general(scaled, coup_all, (((1,), (1,)), ((), ())), preferred_element_type=F32)
    modal3 = modal_late.reshape(modal.shape[0], group, rl)
    lhs, rhs = [scaled_late], [lax.dynamic_index_in_dim(modal3, me, 1, keepdims=False)]
    for d in range(1, group):
        lhs.append(swap(scaled_late, "leafin", d))
        rhs.append(swap(lax.dynamic_index_in_dim(modal3, me ^ d, 1, keepdims=False), "leafin", d))

    half = rows // 2
    piece = half // group
    merged = []
    for h in range(2):
        part = schur[h * half:(h + 1) * half].reshape(2, 2, piece, cols)
        summed = reduce_scatter_2d(part, 1 - h)
        merged.append(unpack(all_gather_2d(summed, 1 - h)).reshape(half, cols))
    merged = jnp.concatenate(merged, axis=0)

    modal_term = jnp.dot(jnp.concatenate(lhs, axis=1), jnp.concatenate(rhs, axis=0), preferred_element_type=F32)

    coords_all = gather_bits(coords, "panel")
    top = lax.reduce_precision(merged, exponent_bits=8, mantissa_bits=7)
    hi, lo = top.astype(BF16), (merged - top).astype(BF16)
    product = jnp.dot(lo, coords_all, preferred_element_type=F32) + jnp.dot(hi, coords_all, preferred_element_type=F32)
    return (modal_term + product)[None]


def solution(mesh):
    def run(*args):
        group = args[5].shape[2] // args[4].shape[2]
        leaves, panels = mesh.shape["leaf"], mesh.shape["panel"]
        grid = mesh.devices.reshape(leaves // group, group, panels)
        sub = Mesh(grid, ("grp", "leafin", "panel"))
        leaf = ("grp", "leafin")
        placed = (
            P(leaf, "panel", None),
            P(leaf, "panel", None),
            P(leaf, None),
            P(leaf),
            P(leaf, "panel", None),
            P(leaf, None, None),
        )
        body = jax.shard_map(on_device, mesh=sub, in_specs=placed, out_specs=P(leaf, "panel", None), check_vma=False)
        return body(*args)

    return run
```
